32 devices in a mesh: row: 4 (over z), col: 4 (over y, x), walk: 2 (over core).
Axes of the slice: x: 2, y: 2, z: 4, core: 2. Of those that a mesh axis runs over, the one named last changes fastest.
Arguments:
- one_elec: bfloat16 [8, 512, 256], P('walk', ('row', 'col')), parts along dimension 0, may hold values from -13 to 13
- pair: bfloat16 [8, 512, 512, 128], P('walk', 'row', 'col'), parts along dimension 0, may hold values from -11 to 11
- spins: int32 [512], replicated, may hold values from 0 to 1, as said below
- w_single: bfloat16 [1024, 256], replicated, may hold values from -0.1875 to 0.1875
- b_single: float32 [256], replicated, may hold values from -1 to 1
- w_pair: bfloat16 [128, 128], replicated, may hold values from -0.5 to 0.5
- w_msg: bfloat16 [256, 128], replicated, may hold values from -0.375 to 0.375
- b_pair: float32 [128], replicated, may hold values from -1 to 1
- d_single: bfloat16 [8, 512, 256], P('walk', ('row', 'col')), parts along dimension 0, may hold values from -13 to 13
- d_pair: bfloat16 [8, 512, 512, 128], P('walk', 'row', 'col'), parts along dimension 0, may hold values from -6 to 6
Outputs:
- single_out: bfloat16 [8, 512, 256], P('walk', ('row', 'col')), parts along dimension 0
- pair_out: bfloat16 [8, 512, 512, 128], P('walk', 'row', 'col'), parts along dimension 0
- grad_single: float32 [8, 512, 256], P('walk', ('row', 'col')), parts along dimension 0
- grad_pair: bfloat16 [8, 512, 512, 128], P('walk', 'row', 'col'), parts along dimension 0
The draws below stay inside these ranges and needn't reach their ends.
There are 2 independent parts, one for each index of `walk`. The reference program is written for one: setup_inputs(seed, part) draws one part's arguments, and reference() takes and returns one part's arrays. A program takes and returns all parts, laid end to end along the dimension named above; an argument that names none is the same for every part. Nothing has to cross between parts.
Inputs may be any that keep to these rules, and one draw needn't show every extreme that they name: `spins`: 1 marks a spin-up electron and 0 a spin-down one; from 128 to 384 electrons are up.
All inputs are finite; a program needn't handle non-finite values.
Results may differ from the reference program's by a relative error of at most 0.005.
Values may be sent and summed in bfloat16 or wider, within the bound.
No kernel may reach another device: no remote copies, remote signals or barrier semaphores. Data moves between devices by JAX's collectives and lax.ppermute only.
A program may use at most 192 MiB of HBM per device.

```python
import jax
import jax.numpy as jnp
from jax import lax

NE = 512
DS = 256
DP = 128
WALK = 4
FIN = 1024


def ramped(key, out_shape, along, off_shape, off_scale):
    base_key, off_key, row_key = jax.random.split(key, 3)
    base_value = jnp.clip(jax.random.normal(base_key, out_shape, jnp.float32), -4.0, 4.0)
    length = out_shape[along]
    ramp_weight = 0.5 + jnp.arange(length).astype(jnp.float32) / float(length)
    ramp_weight = jnp.reshape(ramp_weight, tuple((length if k == along else 1 for k in range(len(out_shape)))))
    offset = jnp.clip(jax.random.normal(off_key, off_shape, jnp.float32), -3.0, 3.0)
    return base_value + off_scale * offset * ramp_weight


def draw_one_elec(key, part):
    return ramped(jax.random.fold_in(key, 11), (WALK, NE, DS), 1, (WALK, 1, DS), 2.0).astype(jnp.bfloat16)


def draw_d_single(key, part):
    return ramped(jax.random.fold_in(key, 23), (WALK, NE, DS), 1, (WALK, 1, DS), 2.0).astype(jnp.bfloat16)


def draw_pair(key, part):
    return ramped(jax.random.fold_in(key, 37), (WALK, NE, NE, DP), 2, (WALK, NE, 1, DP), 1.5).astype(jnp.bfloat16)


def draw_spins(key, part):
    count_key, perm_key = jax.random.split(jax.random.fold_in(key, 51))
    count_up = jax.random.randint(count_key, (), NE // 4, 3 * NE // 4 + 1)
    ranking = jax.random.permutation(perm_key, NE)
    return (ranking < count_up).astype(jnp.int32)


def level_of(own_key, extent, pieces, smallest, largest):
    loudness = 1.0
    for dim, blocks in pieces:
        draws = jax.random.uniform(jax.random.fold_in(jax.random.fold_in(own_key, 6), dim), (blocks,), jnp.float32, smallest / len(pieces), largest / len(pieces))
        loudness = loudness * jnp.repeat(jnp.exp(draws), extent[dim] // blocks).reshape((-1,) + (1,) * (len(extent) - 1 - dim))
    return loudness


def gaussian(stream_key, shape, scale, bound, cuts=(), held_as=jnp.bfloat16):
    values = jax.random.normal(stream_key, shape, jnp.float32) * scale
    if len(cuts) > 0:
        values = level_of(stream_key, shape, cuts, -0.22, 0.18) * values
    return jnp.clip(values, min=-bound, max=bound).astype(held_as)


def setup_inputs(seed: int = 0, part: int = 0) -> dict:
    seeds = jax.random.split(jax.random.key(seed), 11)
    own_keys = jax.random.split(jax.random.fold_in(seeds[10], part), 11)
    one_elec = draw_one_elec(jax.random.fold_in(jax.random.fold_in(seeds[10], part), 71), part)
    pair = draw_pair(jax.random.fold_in(jax.random.fold_in(seeds[10], part), 71), part)
    spins = draw_spins(jax.random.fold_in(seeds[10], 71), part)
    w_single = gaussian(seeds[3], (FIN, DS), FIN ** -0.5, 0.1875)
    b_single = jnp.clip(jax.random.uniform(seeds[4], (DS,), jnp.float32, -1.0, 1.0), -1.0, 1.0)
    w_pair = gaussian(seeds[5], (DP, DP), DP ** -0.5, 0.5)
    w_msg = gaussian(seeds[6], (DS, DP), DS ** -0.5, 0.375)
    b_pair = jnp.clip(jax.random.uniform(seeds[7], (DP,), jnp.float32, -1.0, 1.0), -1.0, 1.0)
    d_single = draw_d_single(jax.random.fold_in(jax.random.fold_in(seeds[10], part), 71), part)
    d_pair = gaussian(own_keys[9], (WALK, NE, NE, DP), 1.0, 6.0, ((1, 4), (2, 4)))
    return dict(one_elec=one_elec, pair=pair, spins=spins, w_single=w_single, b_single=b_single, w_pair=w_pair, w_msg=w_msg, b_pair=b_pair, d_single=d_single, d_pair=d_pair)


def one_walker(single, pair_block, single_cot, pair_cot, spin_up, spin_down, count_up, count_down, w_single, b_single, w_pair, w_msg, b_pair):
    electrons = single.shape[0]
    width_single = single.shape[1]
    width_pair = pair_block.shape[2]
    pair_down = float(electrons) ** -0.75
    pair_boost = float(electrons) ** 0.75
    single_wide = single.astype(jnp.float32)
    pair_wide = pair_block.astype(jnp.float32)
    mean_up = jnp.sum(single_wide * spin_up[:, None], axis=0) / count_up
    mean_down = jnp.sum(single_wide * spin_down[:, None], axis=0) / count_down
    pair_mean_up = jnp.sum(pair_wide * spin_up[None, :, None], axis=1) / count_up
    pair_mean_down = jnp.sum(pair_wide * spin_down[None, :, None], axis=1) / count_down
    features = jnp.concatenate([single_wide, jnp.broadcast_to(mean_up[None, :], (electrons, width_single)), jnp.broadcast_to(mean_down[None, :], (electrons, width_single)), pair_mean_up, pair_mean_down], axis=1).astype(jnp.bfloat16)
    single_act = jnp.tanh(jnp.dot(features, w_single, preferred_element_type=jnp.float32) + b_single)
    single_out = (single_wide + single_act).astype(jnp.bfloat16)
    message = jnp.dot(single, w_msg, preferred_element_type=jnp.float32)
    flat_pair = pair_block.reshape(electrons * electrons, width_pair)
    pre_pair = jnp.dot(flat_pair, w_pair, preferred_element_type=jnp.float32).reshape(electrons, electrons, width_pair) + message[None, :, :] + b_pair
    pair_act = jnp.tanh(pre_pair)
    pair_out = (pair_wide + pair_act).astype(jnp.bfloat16)
    grad_pre = (single_cot.astype(jnp.float32) * (1.0 - single_act * single_act)).astype(jnp.bfloat16)
    feature_grad = jnp.dot(grad_pre, w_single.T, preferred_element_type=jnp.float32)
    grad_direct = feature_grad[:, :width_single]
    grad_mean_up = feature_grad[:, width_single:2 * width_single]
    grad_mean_down = feature_grad[:, 2 * width_single:3 * width_single]
    grad_pm_up = feature_grad[:, 3 * width_single:3 * width_single + width_pair]
    grad_pm_down = feature_grad[:, 3 * width_single + width_pair:]
    pair_delta = (pair_cot.astype(jnp.float32) * (1.0 - pair_act * pair_act)).astype(jnp.bfloat16)
    back_pair = jnp.dot(pair_delta.reshape(electrons * electrons, width_pair), w_pair.T, preferred_element_type=jnp.float32).reshape(electrons, electrons, width_pair)
    spread_pair = spin_up[None, :, None] * (grad_pm_up / count_up)[:, None, :] + spin_down[None, :, None] * (grad_pm_down / count_down)[:, None, :]
    grad_pair = (pair_cot.astype(jnp.float32) + back_pair + pair_boost * spread_pair).astype(jnp.bfloat16)
    column_sum = jnp.sum(pair_delta.astype(jnp.float32), axis=0)
    message_grad = pair_down * jnp.dot(column_sum, w_msg.astype(jnp.float32).T, precision=lax.Precision.HIGHEST)
    mean_grad = spin_up[:, None] * (jnp.sum(grad_mean_up, axis=0) / count_up)[None, :] + spin_down[:, None] * (jnp.sum(grad_mean_down, axis=0) / count_down)[None, :]
    grad_single = single_cot.astype(jnp.float32) + grad_direct + mean_grad + message_grad
    return single_out, pair_out, grad_single, grad_pair


def reference(one_elec, pair, spins, w_single, b_single, w_pair, w_msg, b_pair, d_single, d_pair):
    spin_up = spins.astype(jnp.float32)
    spin_down = 1.0 - spin_up
    count_up = jnp.sum(spin_up)
    count_down = jnp.sum(spin_down)

    def walker_step(walker):
        return one_walker(one_elec[walker], pair[walker], d_single[walker], d_pair[walker], spin_up, spin_down, count_up, count_down, w_single, b_single, w_pair, w_msg, b_pair)

    single_out, pair_out, grad_single, grad_pair = lax.map(walker_step, jnp.arange(WALK))
    return single_out, pair_out, grad_single, grad_pair
```

```python
import jax
import jax.numpy as jnp
from jax import lax
from jax.sharding import PartitionSpec as P

highest = lax.Precision.HIGHEST


def roll_pieces(pieces, shift):
    n = pieces.shape[0]
    doubled = jnp.concatenate([pieces, pieces], axis=0)
    return lax.dynamic_slice_in_dim(doubled, (n - shift) % n, n, 0)


def body(one_elec, pair, spins, w_single, b_single, w_pair, w_msg, b_pair, d_single, d_pair):
    walkers, block_rows, block_cols, width_pair = pair.shape
    own_rows = one_elec.shape[1]
    width_single = one_elec.shape[2]
    electrons = spins.shape[0]
    rows = electrons // block_rows
    cols = electrons // block_cols
    assert rows == cols
    pair_down = float(electrons) ** (-0.75)
    pair_boost = float(electrons) ** 0.75
    row_index = lax.axis_index("row")
    col_index = lax.axis_index("col")
    spin_up = spins.astype(jnp.float32)
    spin_down = 1.0 - spin_up
    count_up = jnp.sum(spin_up)
    count_down = jnp.sum(spin_down)
    counts = jnp.stack([count_up, count_down])
    spin_table = jnp.stack([spin_up, spin_down], axis=1)
    col_start = col_index * block_cols
    own_start = (row_index * cols + col_index) * own_rows
    col_table = lax.dynamic_slice_in_dim(spin_table, col_start, block_cols, 0)
    own_table = lax.dynamic_slice_in_dim(spin_table, own_start, own_rows, 0)

    both = ("row", "col")
    pieces = []
    for s in range(rows):
        perm = [(a * cols + b, ((b - s) % rows) * cols + a) for a in range(rows) for b in range(cols)]
        pieces.append(lax.ppermute(one_elec, both, perm))
    col_single = roll_pieces(jnp.stack(pieces), row_index)
    col_single = jnp.moveaxis(col_single, 0, 1).reshape(walkers, block_cols, width_single)

    col_spin_sums = jnp.einsum(
        "wjd,js->wsd", col_single, col_table.astype(jnp.bfloat16), preferred_element_type=jnp.float32
    )
    partial_value = jnp.einsum(
        "wijd,js->wisd", pair, col_table.astype(jnp.bfloat16), preferred_element_type=jnp.float32
    )
    sub_value = partial_value.reshape(walkers, cols, own_rows, 2, width_pair)
    own_sum = lax.dynamic_index_in_dim(sub_value, col_index, 1, keepdims=False)
    spin_sums = col_spin_sums
    for s in range(1, cols):
        dest = (col_index + s) % cols
        sent = lax.dynamic_index_in_dim(sub_value, dest, 1, keepdims=False)
        payload = jnp.concatenate(
            [sent.reshape(walkers, -1), col_spin_sums.reshape(walkers, -1)], axis=1
        )
        got = lax.ppermute(payload, "col", [(b, (b + s) % cols) for b in range(cols)])
        split = own_rows * 2 * width_pair
        own_sum = own_sum + got[:, :split].reshape(own_sum.shape)
        spin_sums = spin_sums + got[:, split:].reshape(spin_sums.shape)

    spin_means = spin_sums / counts[None, :, None]
    pair_means = own_sum / counts[None, None, :, None]
    single_wide = one_elec.astype(jnp.float32)
    features = jnp.concatenate(
        [
            single_wide,
            jnp.broadcast_to(spin_means[:, None, 0, :], (walkers, own_rows, width_single)),
            jnp.broadcast_to(spin_means[:, None, 1, :], (walkers, own_rows, width_single)),
            pair_means[:, :, 0, :],
            pair_means[:, :, 1, :],
        ],
        axis=2,
    ).astype(jnp.bfloat16)
    single_act = jnp.tanh(
        jnp.einsum("wif,fd->wid", features, w_single, preferred_element_type=jnp.float32) + b_single
    )
    single_out = (single_wide + single_act).astype(jnp.bfloat16)
    grad_pre = (d_single.astype(jnp.float32) * (1.0 - single_act * single_act)).astype(jnp.bfloat16)
    feature_grad = jnp.einsum("wid,fd->wif", grad_pre, w_single, preferred_element_type=jnp.float32)
    grad_direct = feature_grad[:, :, :width_single]
    grad_means = feature_grad[:, :, width_single : 3 * width_single].reshape(
        walkers, own_rows, 2, width_single
    )
    grad_pair_means = feature_grad[:, :, 3 * width_single :].reshape(
        walkers, own_rows, 2, width_pair
    )
    mean_sums = jnp.sum(grad_means, axis=1)

    gathered = [grad_pair_means]
    mean_part = mean_sums
    for s in range(1, cols):
        payload = jnp.concatenate(
            [grad_pair_means.reshape(walkers, -1), mean_sums.reshape(walkers, -1)], axis=1
        )
        got = lax.ppermute(payload, "col", [(b, (b + s) % cols) for b in range(cols)])
        split = own_rows * 2 * width_pair
        gathered.append(got[:, :split].reshape(grad_pair_means.shape))
        mean_part = mean_part + got[:, split:].reshape(mean_sums.shape)
    gathered = jnp.stack(gathered)[::-1]
    gathered = jnp.concatenate([gathered[-1:], gathered[:-1]], axis=0)
    row_pair_grads = roll_pieces(gathered, col_index)
    row_pair_grads = jnp.moveaxis(row_pair_grads, 0, 1).reshape(walkers, block_rows, 2, width_pair)

    message = jnp.einsum("wjd,de->wje", col_single, w_msg, preferred_element_type=jnp.float32)
    pre_pair = (
        jnp.einsum("wijd,de->wije", pair, w_pair, preferred_element_type=jnp.float32)
        + message[:, None, :, :]
        + b_pair
    )
    pair_act = jnp.tanh(pre_pair)
    pair_out = (pair.astype(jnp.float32) + pair_act).astype(jnp.bfloat16)
    col_up = col_table[:, 0]
    col_down = col_table[:, 1]
    spread_pair = (
        col_up[None, None, :, None] * (row_pair_grads[:, :, 0, :] / count_up)[:, :, None, :]
        + col_down[None, None, :, None] * (row_pair_grads[:, :, 1, :] / count_down)[:, :, None, :]
    )
    pair_delta = (d_pair.astype(jnp.float32) * (1.0 - pair_act * pair_act)).astype(jnp.bfloat16)
    back_pair = jnp.einsum("wije,de->wijd", pair_delta, w_pair, preferred_element_type=jnp.float32)
    grad_pair = (d_pair.astype(jnp.float32) + back_pair + pair_boost * spread_pair).astype(
        jnp.bfloat16
    )
    column_sum = jnp.sum(pair_delta, axis=1, dtype=jnp.float32)

    sub_cols = column_sum.reshape(walkers, rows, own_rows, width_pair)
    own_cols = None
    mean_total = None
    for s in range(rows):
        sent = lax.dynamic_index_in_dim(sub_cols, (row_index + s) % rows, 1, keepdims=False)
        payload = jnp.concatenate(
            [sent.reshape(walkers, -1), mean_part.reshape(walkers, -1)], axis=1
        )
        perm = [(a * cols + b, b * cols + (a + s) % rows) for a in range(rows) for b in range(cols)]
        got = lax.ppermute(payload, both, perm)
        split = own_rows * width_pair
        got_cols = got[:, :split].reshape(walkers, own_rows, width_pair)
        got_mean = got[:, split:].reshape(mean_part.shape)
        own_cols = got_cols if own_cols is None else own_cols + got_cols
        mean_total = got_mean if mean_total is None else mean_total + got_mean

    own_message = pair_down * jnp.einsum(
        "wje,de->wjd", own_cols, w_msg.astype(jnp.float32), precision=highest
    )
    own_up = own_table[:, 0]
    own_down = own_table[:, 1]
    electron_grad = (
        own_up[None, :, None] * (mean_total[:, 0, :] / count_up)[:, None, :]
        + own_down[None, :, None] * (mean_total[:, 1, :] / count_down)[:, None, :]
        + own_message
    )
    grad_single = d_single.astype(jnp.float32) + grad_direct + electron_grad
    return (single_out, pair_out, grad_single, grad_pair)


def solution(mesh):
    placed = (
        P("walk", ("row", "col"), None),
        P("walk", "row", "col", None),
        P(),
        P(),
        P(),
        P(),
        P(),
        P(),
        P("walk", ("row", "col"), None),
        P("walk", "row", "col", None),
    )
    return jax.shard_map(
        body,
        mesh=mesh,
        in_specs=placed,
        out_specs=(
            P("walk", ("row", "col"), None),
            P("walk", "row", "col", None),
            P("walk", ("row", "col"), None),
            P("walk", "row", "col", None),
        ),
        check_vma=False,
    )
```

```python
import jax
import jax.numpy as jnp
from jax import lax
from jax.experimental import pallas as pl
from jax.experimental.pallas import tpu as pltpu
from jax.sharding import PartitionSpec as P

def pair_kernel(pair_ref, dpair_ref, msg_ref, wp_ref, wpt_ref, b_ref, mask_ref, aup_ref, adn_ref,
                out_ref, grad_ref, col_ref):
    i = pl.program_id(1)
    ti, bc, dp = pair_ref.shape[1:]
    x = pair_ref[0]
    pre = jnp.dot(x.reshape(ti * bc, dp), wp_ref[...], preferred_element_type=jnp.float32)
    pre = pre.reshape(ti, bc, dp) + msg_ref[0][None] + b_ref[...][None]
    act = jnp.tanh(pre)
    out_ref[0] = (x.astype(jnp.float32) + act).astype(out_ref.dtype)
    d = dpair_ref[0].astype(jnp.float32)
    delta = (d * (1.0 - act * act)).astype(jnp.bfloat16)
    back = jnp.dot(delta.reshape(ti * bc, dp), wpt_ref[...], preferred_element_type=jnp.float32)
    spread = jnp.where(mask_ref[...][None] > 0.5, aup_ref[0][:, None, :], adn_ref[0][:, None, :])
    grad_ref[0] = (d + back.reshape(ti, bc, dp) + spread).astype(grad_ref.dtype)
    part = jnp.sum(delta.astype(jnp.float32), axis=0)

    @pl.when(i == 0)
    def _():
        col_ref[0] = part

    @pl.when(i > 0)
    def _():
        col_ref[0] = col_ref[0] + part


def pair_pass(pair, d_pair, message_b, w_pair, b_pair, up_mask, a_up, a_down, interpret=False):
    w, br, bc, dp = pair.shape
    ti = max(1, min(br, 2048 // bc))
    grid = (w, br // ti)
    blk = pl.BlockSpec((1, ti, bc, dp), lambda a, i: (a, i, 0, 0))
    whole2 = lambda shape: pl.BlockSpec(shape, lambda a, i: (0, 0))
    per_w = pl.BlockSpec((1, bc, dp), lambda a, i: (a, 0, 0))
    rows = pl.BlockSpec((1, ti, dp), lambda a, i: (a, i, 0))
    return pl.pallas_call(
        pair_kernel,
        grid=grid,
        in_specs=[blk, blk, per_w, whole2((dp, dp)), whole2((dp, dp)), whole2((1, dp)),
                  whole2((bc, dp)), rows, rows],
        out_specs=[blk, blk, per_w],
        out_shape=[jax.ShapeDtypeStruct(pair.shape, jnp.bfloat16),
                   jax.ShapeDtypeStruct(pair.shape, jnp.bfloat16),
                   jax.ShapeDtypeStruct((w, bc, dp), jnp.float32)],
        compiler_params=pltpu.CompilerParams(dimension_semantics=("arbitrary", "arbitrary")),
        interpret=interpret,
    )(pair, d_pair, message_b, w_pair, w_pair.T, b_pair.reshape(1, dp), up_mask, a_up, a_down)

highest = lax.Precision.HIGHEST


def roll_pieces(pieces, shift):
    n = pieces.shape[0]
    doubled = jnp.concatenate([pieces, pieces], axis=0)
    return lax.dynamic_slice_in_dim(doubled, (n - shift) % n, n, 0)


def body(one_elec, pair, spins, w_single, b_single, w_pair, w_msg, b_pair, d_single, d_pair):
    walkers, block_rows, block_cols, width_pair = pair.shape
    own_rows = one_elec.shape[1]
    width_single = one_elec.shape[2]
    electrons = spins.shape[0]
    rows = electrons // block_rows
    cols = electrons // block_cols
    assert rows == cols
    pair_down = float(electrons) ** (-0.75)
    pair_boost = float(electrons) ** 0.75
    row_index = lax.axis_index("row")
    col_index = lax.axis_index("col")
    spin_up = spins.astype(jnp.float32)
    spin_down = 1.0 - spin_up
    count_up = jnp.sum(spin_up)
    count_down = jnp.sum(spin_down)
    counts = jnp.stack([count_up, count_down])
    spin_table = jnp.stack([spin_up, spin_down], axis=1)
    col_start = col_index * block_cols
    own_start = (row_index * cols + col_index) * own_rows
    col_table = lax.dynamic_slice_in_dim(spin_table, col_start, block_cols, 0)
    own_table = lax.dynamic_slice_in_dim(spin_table, own_start, own_rows, 0)
    both = ("row", "col")

    own_pack = jnp.concatenate([one_elec, d_single], axis=2)
    pieces = [own_pack]
    for s in range(1, cols):
        pieces.append(lax.ppermute(own_pack, "col", [(b, (b + s) % cols) for b in range(cols)]))
    pieces = jnp.stack(pieces)
    pieces = jnp.concatenate([pieces[:1], pieces[1:][::-1]], axis=0)
    row_pack = roll_pieces(pieces, col_index)
    row_pack = jnp.moveaxis(row_pack, 0, 1).reshape(walkers, block_rows, 2 * width_single)
    row_single = row_pack[:, :, :width_single]
    row_cot = row_pack[:, :, width_single:]

    col_single = lax.ppermute(
        row_single, both, [(a * cols + b, b * cols + a) for a in range(rows) for b in range(cols)]
    )

    partial_value = jnp.einsum(
        "wijd,js->wisd", pair, col_table.astype(jnp.bfloat16), preferred_element_type=jnp.float32
    )
    col_spin_sums = jnp.einsum(
        "wjd,js->wsd", col_single, col_table.astype(jnp.bfloat16), preferred_element_type=jnp.float32
    )
    spin_hi = col_spin_sums.astype(jnp.bfloat16)
    spin_lo = (col_spin_sums - spin_hi.astype(jnp.float32)).astype(jnp.bfloat16)
    payload = jnp.concatenate(
        [
            partial_value.astype(jnp.bfloat16).reshape(walkers, -1),
            spin_hi.reshape(walkers, -1),
            spin_lo.reshape(walkers, -1),
        ],
        axis=1,
    )
    split = block_rows * 2 * width_pair
    spin_size = 2 * width_single
    row_sum = partial_value
    spin_sums = col_spin_sums
    for s in range(1, cols):
        got = lax.ppermute(payload, "col", [(b, (b + s) % cols) for b in range(cols)])
        row_sum = row_sum + got[:, :split].astype(jnp.float32).reshape(row_sum.shape)
        got_hi = got[:, split : split + spin_size].astype(jnp.float32)
        got_lo = got[:, split + spin_size :].astype(jnp.float32)
        spin_sums = spin_sums + (got_hi + got_lo).reshape(spin_sums.shape)

    spin_means = spin_sums / counts[None, :, None]
    pair_means = row_sum / counts[None, None, :, None]
    single_wide = row_single.astype(jnp.float32)
    features = jnp.concatenate(
        [
            single_wide,
            jnp.broadcast_to(spin_means[:, None, 0, :], (walkers, block_rows, width_single)),
            jnp.broadcast_to(spin_means[:, None, 1, :], (walkers, block_rows, width_single)),
            pair_means[:, :, 0, :],
            pair_means[:, :, 1, :],
        ],
        axis=2,
    ).astype(jnp.bfloat16)
    single_act = jnp.tanh(
        jnp.einsum("wif,fd->wid", features, w_single, preferred_element_type=jnp.float32) + b_single
    )
    single_all = (single_wide + single_act).astype(jnp.bfloat16)
    grad_pre = (row_cot.astype(jnp.float32) * (1.0 - single_act * single_act)).astype(jnp.bfloat16)
    feature_grad = jnp.einsum("wid,fd->wif", grad_pre, w_single, preferred_element_type=jnp.float32)
    grad_means = feature_grad[:, :, width_single : 3 * width_single].reshape(
        walkers, block_rows, 2, width_single
    )
    row_pair_grads = feature_grad[:, :, 3 * width_single :].reshape(
        walkers, block_rows, 2, width_pair
    )
    mean_part = jnp.sum(grad_means, axis=1)
    own_offset = col_index * own_rows
    single_out = lax.dynamic_slice_in_dim(single_all, own_offset, own_rows, 1)
    grad_direct = lax.dynamic_slice_in_dim(feature_grad[:, :, :width_single], own_offset, own_rows, 1)

    message = jnp.einsum("wjd,de->wje", col_single, w_msg, preferred_element_type=jnp.float32)
    a_up = pair_boost * (row_pair_grads[:, :, 0, :] / count_up)
    a_down = pair_boost * (row_pair_grads[:, :, 1, :] / count_down)
    up_mask = jnp.broadcast_to(col_table[:, :1], (block_cols, width_pair))
    pair_out, grad_pair, column_sum = pair_pass(
        pair, d_pair, message, w_pair, b_pair, up_mask, a_up, a_down
    )

    sub_cols = column_sum.reshape(walkers, rows, own_rows, width_pair)
    own_cols = None
    mean_total = None
    for s in range(rows):
        sent = lax.dynamic_index_in_dim(sub_cols, (row_index + s) % rows, 1, keepdims=False)
        payload = jnp.concatenate(
            [sent.reshape(walkers, -1), mean_part.reshape(walkers, -1)], axis=1
        )
        perm = [(a * cols + b, b * cols + (a + s) % rows) for a in range(rows) for b in range(cols)]
        got = lax.ppermute(payload, both, perm)
        split = own_rows * width_pair
        got_cols = got[:, :split].reshape(walkers, own_rows, width_pair)
        got_mean = got[:, split:].reshape(mean_part.shape)
        own_cols = got_cols if own_cols is None else own_cols + got_cols
        mean_total = got_mean if mean_total is None else mean_total + got_mean

    own_message = pair_down * jnp.einsum(
        "wje,de->wjd", own_cols, w_msg.astype(jnp.float32), precision=highest
    )
    own_up = own_table[:, 0]
    own_down = own_table[:, 1]
    electron_grad = (
        own_up[None, :, None] * (mean_total[:, 0, :] / count_up)[:, None, :]
        + own_down[None, :, None] * (mean_total[:, 1, :] / count_down)[:, None, :]
        + own_message
    )
    grad_single = d_single.astype(jnp.float32) + grad_direct + electron_grad
    return (single_out, pair_out, grad_single, grad_pair)


def solution(mesh):
    placed = (
        P("walk", ("row", "col"), None),
        P("walk", "row", "col", None),
        P(),
        P(),
        P(),
        P(),
        P(),
        P(),
        P("walk", ("row", "col"), None),
        P("walk", "row", "col", None),
    )
    return jax.shard_map(
        body,
        mesh=mesh,
        in_specs=placed,
        out_specs=(
            P("walk", ("row", "col"), None),
            P("walk", "row", "col", None),
            P("walk", ("row", "col"), None),
            P("walk", "row", "col", None),
        ),
        check_vma=False,
    )
```

```python
import jax
import jax.numpy as jnp
from jax import lax
from jax.experimental import pallas as pl
from jax.experimental.pallas import tpu as pltpu
from jax.sharding import PartitionSpec as P

def pair_kernel(pair_ref, dpair_ref, msg_ref, wp_ref, wpt_ref, b_ref, mask_ref, aup_ref, adn_ref,
                *rest):
    out_ref, grad_ref, col_ref = rest[-3:]
    i = pl.program_id(1)
    ti, bc, dp = pair_ref.shape[1:]
    x = pair_ref[0]
    pre = jnp.dot(x.reshape(ti * bc, dp), wp_ref[...], preferred_element_type=jnp.float32)
    pre = pre.reshape(ti, bc, dp) + msg_ref[0][None] + b_ref[...][None]
    act = jnp.tanh(pre)
    out_ref[0] = (x.astype(jnp.float32) + act).astype(out_ref.dtype)
    d = dpair_ref[0].astype(jnp.float32)
    delta = (d * (1.0 - act * act)).astype(jnp.bfloat16)
    back = jnp.dot(delta.reshape(ti * bc, dp), wpt_ref[...], preferred_element_type=jnp.float32)
    spread = jnp.where(mask_ref[...][None] > 0.5, aup_ref[0][:, None, :], adn_ref[0][:, None, :])
    grad_ref[0] = (d + back.reshape(ti, bc, dp) + spread).astype(grad_ref.dtype)
    part = jnp.sum(delta.astype(jnp.float32), axis=0)

    @pl.when(i == 0)
    def _():
        col_ref[0] = part

    @pl.when(i > 0)
    def _():
        col_ref[0] = col_ref[0] + part


def pair_pass(pair, d_pair, message_b, w_pair, b_pair, up_mask, a_up, a_down, first, prev=None):
    w, br, bc, dp = pair.shape
    group = message_b.shape[0]
    ti = max(1, min(br, 2048 // bc))
    grid = (group, br // ti)
    blk = pl.BlockSpec((1, ti, bc, dp), lambda a, i: (a + first, i, 0, 0))
    whole2 = lambda shape: pl.BlockSpec(shape, lambda a, i: (0, 0))
    per_w = pl.BlockSpec((1, bc, dp), lambda a, i: (a, 0, 0))
    rows = pl.BlockSpec((1, ti, dp), lambda a, i: (a, i, 0))
    in_specs = [blk, blk, per_w, whole2((dp, dp)), whole2((dp, dp)), whole2((1, dp)),
                whole2((bc, dp)), rows, rows]
    args = [pair, d_pair, message_b, w_pair, w_pair.T, b_pair.reshape(1, dp), up_mask, a_up, a_down]
    aliases = {}
    if prev is not None:
        in_specs += [pl.BlockSpec(memory_space=pl.ANY), pl.BlockSpec(memory_space=pl.ANY)]
        aliases = {len(args): 0, len(args) + 1: 1}
        args += list(prev)
    return pl.pallas_call(
        pair_kernel,
        grid=grid,
        in_specs=in_specs,
        out_specs=[blk, blk, per_w],
        out_shape=[jax.ShapeDtypeStruct(pair.shape, jnp.bfloat16),
                   jax.ShapeDtypeStruct(pair.shape, jnp.bfloat16),
                   jax.ShapeDtypeStruct((group, bc, dp), jnp.float32)],
        input_output_aliases=aliases,
        cost_estimate=pl.CostEstimate(
            flops=4 * group * br * bc * dp * dp,
            transcendentals=group * br * bc * dp,
            bytes_accessed=8 * group * br * bc * dp,
        ),
        compiler_params=pltpu.CompilerParams(dimension_semantics=("arbitrary", "arbitrary")),
    )(*args)


highest = lax.Precision.HIGHEST


def roll_pieces(pieces, shift):
    n = pieces.shape[0]
    doubled = jnp.concatenate([pieces, pieces], axis=0)
    return lax.dynamic_slice_in_dim(doubled, (n - shift) % n, n, 0)


def body(one_elec, pair, spins, w_single, b_single, w_pair, w_msg, b_pair, d_single, d_pair):
    walkers, block_rows, block_cols, width_pair = pair.shape
    own_rows = one_elec.shape[1]
    width_single = one_elec.shape[2]
    electrons = spins.shape[0]
    rows = electrons // block_rows
    cols = electrons // block_cols
    assert rows == cols
    pair_down = float(electrons) ** (-0.75)
    pair_boost = float(electrons) ** 0.75
    row_index = lax.axis_index("row")
    col_index = lax.axis_index("col")
    spin_up = spins.astype(jnp.float32)
    spin_down = 1.0 - spin_up
    count_up = jnp.sum(spin_up)
    count_down = jnp.sum(spin_down)
    counts = jnp.stack([count_up, count_down])
    spin_table = jnp.stack([spin_up, spin_down], axis=1)
    col_start = col_index * block_cols
    own_start = (row_index * cols + col_index) * own_rows
    col_table = lax.dynamic_slice_in_dim(spin_table, col_start, block_cols, 0)
    own_table = lax.dynamic_slice_in_dim(spin_table, own_start, own_rows, 0)

    both = ("row", "col")
    pieces = []
    for s in range(rows):
        perm = [(a * cols + b, ((b - s) % rows) * cols + a) for a in range(rows) for b in range(cols)]
        pieces.append(lax.ppermute(one_elec, both, perm))
    col_single = roll_pieces(jnp.stack(pieces), row_index)
    col_single = jnp.moveaxis(col_single, 0, 1).reshape(walkers, block_cols, width_single)

    col_spin_sums = jnp.einsum(
        "wjd,js->wsd", col_single, col_table.astype(jnp.bfloat16), preferred_element_type=jnp.float32
    )
    partial_value = jnp.einsum(
        "wijd,js->wisd", pair, col_table.astype(jnp.bfloat16), preferred_element_type=jnp.float32
    )
    sub_value = partial_value.reshape(walkers, cols, own_rows, 2, width_pair)
    own_sum = lax.dynamic_index_in_dim(sub_value, col_index, 1, keepdims=False)
    spin_sums = col_spin_sums
    spin_hi = col_spin_sums.astype(jnp.bfloat16)
    spin_lo = (col_spin_sums - spin_hi.astype(jnp.float32)).astype(jnp.bfloat16)
    split = own_rows * 2 * width_pair
    spin_size = 2 * width_single
    for s in range(1, cols):
        dest = col_index ^ s
        sent = lax.dynamic_index_in_dim(sub_value, dest, 1, keepdims=False)
        payload = jnp.concatenate(
            [
                sent.astype(jnp.bfloat16).reshape(walkers, -1),
                spin_hi.reshape(walkers, -1),
                spin_lo.reshape(walkers, -1),
            ],
            axis=1,
        )
        got = lax.ppermute(payload, "col", [(b, b ^ s) for b in range(cols)])
        own_sum = own_sum + got[:, :split].astype(jnp.float32).reshape(own_sum.shape)
        got_hi = got[:, split : split + spin_size].astype(jnp.float32)
        got_lo = got[:, split + spin_size :].astype(jnp.float32)
        spin_sums = spin_sums + (got_hi + got_lo).reshape(spin_sums.shape)

    spin_means = spin_sums / counts[None, :, None]
    pair_means = own_sum / counts[None, None, :, None]
    single_wide = one_elec.astype(jnp.float32)
    features = jnp.concatenate(
        [
            single_wide,
            jnp.broadcast_to(spin_means[:, None, 0, :], (walkers, own_rows, width_single)),
            jnp.broadcast_to(spin_means[:, None, 1, :], (walkers, own_rows, width_single)),
            pair_means[:, :, 0, :],
            pair_means[:, :, 1, :],
        ],
        axis=2,
    ).astype(jnp.bfloat16)
    single_act = jnp.tanh(
        jnp.einsum("wif,fd->wid", features, w_single, preferred_element_type=jnp.float32) + b_single
    )
    single_out = (single_wide + single_act).astype(jnp.bfloat16)
    grad_pre = (d_single.astype(jnp.float32) * (1.0 - single_act * single_act)).astype(jnp.bfloat16)
    feature_grad = jnp.einsum("wid,fd->wif", grad_pre, w_single, preferred_element_type=jnp.float32)
    grad_direct = feature_grad[:, :, :width_single]
    grad_means = feature_grad[:, :, width_single : 3 * width_single].reshape(
        walkers, own_rows, 2, width_single
    )
    grad_pair_means = feature_grad[:, :, 3 * width_single :].reshape(
        walkers, own_rows, 2, width_pair
    )
    mean_sums = jnp.sum(grad_means, axis=1)

    mean_hi = mean_sums.astype(jnp.bfloat16)
    mean_lo = (mean_sums - mean_hi.astype(jnp.float32)).astype(jnp.bfloat16)
    payload = jnp.concatenate(
        [
            grad_pair_means.astype(jnp.bfloat16).reshape(walkers, -1),
            mean_hi.reshape(walkers, -1),
            mean_lo.reshape(walkers, -1),
        ],
        axis=1,
    )
    split = own_rows * 2 * width_pair
    mean_size = 2 * width_single
    gathered = [grad_pair_means.astype(jnp.bfloat16).astype(jnp.float32)] + [None] * (cols - 1)
    mean_part = mean_sums
    for s in range(1, cols):
        got = lax.ppermute(payload, "col", [(b, b ^ s) for b in range(cols)])
        gathered[s] = got[:, :split].astype(jnp.float32).reshape(grad_pair_means.shape)
        got_hi = got[:, split : split + mean_size].astype(jnp.float32)
        got_lo = got[:, split + mean_size :].astype(jnp.float32)
        mean_part = mean_part + (got_hi + got_lo).reshape(mean_sums.shape)
    gathered = jnp.stack(gathered)
    order = jnp.arange(cols) ^ col_index
    row_pair_grads = jnp.take(gathered, order, axis=0)
    row_pair_grads = jnp.moveaxis(row_pair_grads, 0, 1).reshape(walkers, block_rows, 2, width_pair)

    message = jnp.einsum("wjd,de->wje", col_single, w_msg, preferred_element_type=jnp.float32)
    a_up = pair_boost * (row_pair_grads[:, :, 0, :] / count_up)
    a_down = pair_boost * (row_pair_grads[:, :, 1, :] / count_down)
    up_mask = jnp.broadcast_to(col_table[:, :1], (block_cols, width_pair))
    pair_out, grad_pair, column_sum = pair_pass(
        pair, d_pair, message, w_pair, b_pair, up_mask, a_up, a_down, 0
    )

    sub_cols = column_sum.reshape(walkers, rows, own_rows, width_pair)
    mean_hi = mean_part.astype(jnp.bfloat16)
    mean_lo = (mean_part - mean_hi.astype(jnp.float32)).astype(jnp.bfloat16)
    split = own_rows * width_pair
    mean_size = 2 * width_single
    own_cols = None
    mean_total = None
    for s in range(rows):
        sent = lax.dynamic_index_in_dim(sub_cols, (row_index + s) % rows, 1, keepdims=False)
        payload = jnp.concatenate(
            [
                sent.astype(jnp.bfloat16).reshape(walkers, -1),
                mean_hi.reshape(walkers, -1),
                mean_lo.reshape(walkers, -1),
            ],
            axis=1,
        )
        perm = [(a * cols + b, b * cols + (a + s) % rows) for a in range(rows) for b in range(cols)]
        got = lax.ppermute(payload, both, perm)
        got_cols = got[:, :split].astype(jnp.float32).reshape(walkers, own_rows, width_pair)
        got_hi = got[:, split : split + mean_size].astype(jnp.float32)
        got_lo = got[:, split + mean_size :].astype(jnp.float32)
        got_mean = (got_hi + got_lo).reshape(mean_part.shape)
        own_cols = got_cols if own_cols is None else own_cols + got_cols
        mean_total = got_mean if mean_total is None else mean_total + got_mean

    own_message = pair_down * jnp.einsum(
        "wje,de->wjd", own_cols, w_msg.astype(jnp.float32), precision=highest
    )
    own_up = own_table[:, 0]
    own_down = own_table[:, 1]
    electron_grad = (
        own_up[None, :, None] * (mean_total[:, 0, :] / count_up)[:, None, :]
        + own_down[None, :, None] * (mean_total[:, 1, :] / count_down)[:, None, :]
        + own_message
    )
    grad_single = d_single.astype(jnp.float32) + grad_direct + electron_grad
    return (single_out, pair_out, grad_single, grad_pair)


def solution(mesh):
    placed = (
        P("walk", ("row", "col"), None),
        P("walk", "row", "col", None),
        P(),
        P(),
        P(),
        P(),
        P(),
        P(),
        P("walk", ("row", "col"), None),
        P("walk", "row", "col", None),
    )
    return jax.shard_map(
        body,
        mesh=mesh,
        in_specs=placed,
        out_specs=(
            P("walk", ("row", "col"), None),
            P("walk", "row", "col", None),
            P("walk", ("row", "col"), None),
            P("walk", "row", "col", None),
        ),
        check_vma=False,
    )
```

```python
import jax
import jax.numpy as jnp
from jax import lax
from jax.experimental import pallas as pl
from jax.experimental.pallas import tpu as pltpu
from jax.sharding import PartitionSpec as P

def pair_kernel(pair_ref, dpair_ref, msg_ref, wp_ref, wpt_ref, b_ref, mask_ref, aup_ref, adn_ref,
                *rest):
    out_ref, grad_ref, col_ref = rest[-3:]
    i = pl.program_id(1)
    ti, bc, dp = pair_ref.shape[1:]
    x = pair_ref[0]
    pre = jnp.dot(x.reshape(ti * bc, dp), wp_ref[...], preferred_element_type=jnp.float32)
    pre = pre.reshape(ti, bc, dp) + msg_ref[0][None] + b_ref[...][None]
    act = jnp.tanh(pre)
    out_ref[0] = (x.astype(jnp.float32) + act).astype(out_ref.dtype)
    d = dpair_ref[0].astype(jnp.float32)
    delta = (d * (1.0 - act * act)).astype(jnp.bfloat16)
    back = jnp.dot(delta.reshape(ti * bc, dp), wpt_ref[...], preferred_element_type=jnp.float32)
    spread = jnp.where(mask_ref[...][None] > 0.5, aup_ref[0][:, None, :], adn_ref[0][:, None, :])
    grad_ref[0] = (d + back.reshape(ti, bc, dp) + spread).astype(grad_ref.dtype)
    part = jnp.sum(delta.astype(jnp.float32), axis=0)

    @pl.when(i == 0)
    def _():
        col_ref[0] = part

    @pl.when(i > 0)
    def _():
        col_ref[0] = col_ref[0] + part


def pair_pass(pair, d_pair, message_b, w_pair, b_pair, up_mask, a_up, a_down, first, prev=None):
    w, br, bc, dp = pair.shape
    group = message_b.shape[0]
    ti = max(1, min(br, 2048 // bc))
    grid = (group, br // ti)
    blk = pl.BlockSpec((1, ti, bc, dp), lambda a, i: (a + first, i, 0, 0))
    whole2 = lambda shape: pl.BlockSpec(shape, lambda a, i: (0, 0))
    per_w = pl.BlockSpec((1, bc, dp), lambda a, i: (a, 0, 0))
    rows = pl.BlockSpec((1, ti, dp), lambda a, i: (a, i, 0))
    in_specs = [blk, blk, per_w, whole2((dp, dp)), whole2((dp, dp)), whole2((1, dp)),
                whole2((bc, dp)), rows, rows]
    args = [pair, d_pair, message_b, w_pair, w_pair.T, b_pair.reshape(1, dp), up_mask, a_up, a_down]
    aliases = {}
    if prev is not None:
        in_specs += [pl.BlockSpec(memory_space=pl.ANY), pl.BlockSpec(memory_space=pl.ANY)]
        aliases = {len(args): 0, len(args) + 1: 1}
        args += list(prev)
    return pl.pallas_call(
        pair_kernel,
        grid=grid,
        in_specs=in_specs,
        out_specs=[blk, blk, per_w],
        out_shape=[jax.ShapeDtypeStruct(pair.shape, jnp.bfloat16),
                   jax.ShapeDtypeStruct(pair.shape, jnp.bfloat16),
                   jax.ShapeDtypeStruct((group, bc, dp), jnp.float32)],
        input_output_aliases=aliases,
        cost_estimate=pl.CostEstimate(
            flops=4 * group * br * bc * dp * dp,
            transcendentals=group * br * bc * dp,
            bytes_accessed=8 * group * br * bc * dp,
        ),
        compiler_params=pltpu.CompilerParams(dimension_semantics=("arbitrary", "arbitrary")),
    )(*args)


highest = lax.Precision.HIGHEST


def roll_pieces(pieces, shift):
    n = pieces.shape[0]
    doubled = jnp.concatenate([pieces, pieces], axis=0)
    return lax.dynamic_slice_in_dim(doubled, (n - shift) % n, n, 0)


def body(one_elec, pair, spins, w_single, b_single, w_pair, w_msg, b_pair, d_single, d_pair):
    walkers, block_rows, block_cols, width_pair = pair.shape
    own_rows = one_elec.shape[1]
    width_single = one_elec.shape[2]
    electrons = spins.shape[0]
    rows = electrons // block_rows
    cols = electrons // block_cols
    assert rows == cols
    pair_down = float(electrons) ** (-0.75)
    pair_boost = float(electrons) ** 0.75
    row_index = lax.axis_index("row")
    col_index = lax.axis_index("col")
    spin_up = spins.astype(jnp.float32)
    spin_down = 1.0 - spin_up
    count_up = jnp.sum(spin_up)
    count_down = jnp.sum(spin_down)
    counts = jnp.stack([count_up, count_down])
    spin_table = jnp.stack([spin_up, spin_down], axis=1)
    col_start = col_index * block_cols
    own_start = (row_index * cols + col_index) * own_rows
    col_table = lax.dynamic_slice_in_dim(spin_table, col_start, block_cols, 0)
    own_table = lax.dynamic_slice_in_dim(spin_table, own_start, own_rows, 0)

    both = ("row", "col")
    pieces = []
    for s in range(rows):
        perm = [(a * cols + b, ((b - s) % rows) * cols + a) for a in range(rows) for b in range(cols)]
        pieces.append(lax.ppermute(one_elec, both, perm))
    col_single = roll_pieces(jnp.stack(pieces), row_index)
    col_single = jnp.moveaxis(col_single, 0, 1).reshape(walkers, block_cols, width_single)

    col_spin_sums = jnp.einsum(
        "wjd,js->wsd", col_single, col_table.astype(jnp.bfloat16), preferred_element_type=jnp.float32
    )
    partial_value = jnp.einsum(
        "wijd,js->wisd", pair, col_table.astype(jnp.bfloat16), preferred_element_type=jnp.float32
    )
    spin_hi = col_spin_sums.astype(jnp.bfloat16)
    spin_lo = (col_spin_sums - spin_hi.astype(jnp.float32)).astype(jnp.bfloat16)
    split = own_rows * 2 * width_pair
    spin_size = 2 * width_single
    sub_value = jnp.moveaxis(partial_value.reshape(walkers, cols, own_rows, 2, width_pair), 1, 0)
    spin_pack = jnp.concatenate([spin_hi.reshape(walkers, -1), spin_lo.reshape(walkers, -1)], axis=1)
    payload = jnp.concatenate(
        [
            sub_value.astype(jnp.bfloat16).reshape(cols, walkers, -1),
            jnp.broadcast_to(spin_pack[None], (cols, walkers, 2 * spin_size)),
        ],
        axis=2,
    )
    got = lax.all_to_all(payload, "col", 0, 0, tiled=True).astype(jnp.float32)
    own_sum = jnp.sum(got[:, :, :split], axis=0).reshape(walkers, own_rows, 2, width_pair)
    spin_got = got[:, :, split:]
    spin_sums = jnp.sum(spin_got[:, :, :spin_size] + spin_got[:, :, spin_size:], axis=0).reshape(
        col_spin_sums.shape
    )

    spin_means = spin_sums / counts[None, :, None]
    pair_means = own_sum / counts[None, None, :, None]
    single_wide = one_elec.astype(jnp.float32)
    features = jnp.concatenate(
        [
            single_wide,
            jnp.broadcast_to(spin_means[:, None, 0, :], (walkers, own_rows, width_single)),
            jnp.broadcast_to(spin_means[:, None, 1, :], (walkers, own_rows, width_single)),
            pair_means[:, :, 0, :],
            pair_means[:, :, 1, :],
        ],
        axis=2,
    ).astype(jnp.bfloat16)
    single_act = jnp.tanh(
        jnp.einsum("wif,fd->wid", features, w_single, preferred_element_type=jnp.float32) + b_single
    )
    single_out = (single_wide + single_act).astype(jnp.bfloat16)
    grad_pre = (d_single.astype(jnp.float32) * (1.0 - single_act * single_act)).astype(jnp.bfloat16)
    feature_grad = jnp.einsum("wid,fd->wif", grad_pre, w_single, preferred_element_type=jnp.float32)
    grad_direct = feature_grad[:, :, :width_single]
    grad_means = feature_grad[:, :, width_single : 3 * width_single].reshape(
        walkers, own_rows, 2, width_single
    )
    grad_pair_means = feature_grad[:, :, 3 * width_single :].reshape(
        walkers, own_rows, 2, width_pair
    )
    mean_sums = jnp.sum(grad_means, axis=1)

    mean_hi = mean_sums.astype(jnp.bfloat16)
    mean_lo = (mean_sums - mean_hi.astype(jnp.float32)).astype(jnp.bfloat16)
    payload = jnp.concatenate(
        [
            grad_pair_means.astype(jnp.bfloat16).reshape(walkers, -1),
            mean_hi.reshape(walkers, -1),
            mean_lo.reshape(walkers, -1),
        ],
        axis=1,
    )
    split = own_rows * 2 * width_pair
    mean_size = 2 * width_single
    got = lax.all_to_all(
        jnp.broadcast_to(payload[None], (cols,) + payload.shape), "col", 0, 0, tiled=True
    ).astype(jnp.float32)
    row_pair_grads = got[:, :, :split].reshape(cols, walkers, own_rows, 2, width_pair)
    row_pair_grads = jnp.moveaxis(row_pair_grads, 0, 1).reshape(walkers, block_rows, 2, width_pair)
    mean_got = got[:, :, split:]
    mean_part = jnp.sum(mean_got[:, :, :mean_size] + mean_got[:, :, mean_size:], axis=0).reshape(
        mean_sums.shape
    )

    message = jnp.einsum("wjd,de->wje", col_single, w_msg, preferred_element_type=jnp.float32)
    a_up = pair_boost * (row_pair_grads[:, :, 0, :] / count_up)
    a_down = pair_boost * (row_pair_grads[:, :, 1, :] / count_down)
    up_mask = jnp.broadcast_to(col_table[:, :1], (block_cols, width_pair))
    pair_out, grad_pair, column_sum = pair_pass(
        pair, d_pair, message, w_pair, b_pair, up_mask, a_up, a_down, 0
    )

    sub_cols = column_sum.reshape(walkers, rows, own_rows, width_pair)
    mean_hi = mean_part.astype(jnp.bfloat16)
    mean_lo = (mean_part - mean_hi.astype(jnp.float32)).astype(jnp.bfloat16)
    split = own_rows * width_pair
    mean_size = 2 * width_single
    own_cols = None
    mean_total = None
    for s in range(rows):
        sent = lax.dynamic_index_in_dim(sub_cols, (row_index + s) % rows, 1, keepdims=False)
        payload = jnp.concatenate(
            [
                sent.astype(jnp.bfloat16).reshape(walkers, -1),
                mean_hi.reshape(walkers, -1),
                mean_lo.reshape(walkers, -1),
            ],
            axis=1,
        )
        perm = [(a * cols + b, b * cols + (a + s) % rows) for a in range(rows) for b in range(cols)]
        got = lax.ppermute(payload, both, perm)
        got_cols = got[:, :split].astype(jnp.float32).reshape(walkers, own_rows, width_pair)
        got_hi = got[:, split : split + mean_size].astype(jnp.float32)
        got_lo = got[:, split + mean_size :].astype(jnp.float32)
        got_mean = (got_hi + got_lo).reshape(mean_part.shape)
        own_cols = got_cols if own_cols is None else own_cols + got_cols
        mean_total = got_mean if mean_total is None else mean_total + got_mean

    own_message = pair_down * jnp.einsum(
        "wje,de->wjd", own_cols, w_msg.astype(jnp.float32), precision=highest
    )
    own_up = own_table[:, 0]
    own_down = own_table[:, 1]
    electron_grad = (
        own_up[None, :, None] * (mean_total[:, 0, :] / count_up)[:, None, :]
        + own_down[None, :, None] * (mean_total[:, 1, :] / count_down)[:, None, :]
        + own_message
    )
    grad_single = d_single.astype(jnp.float32) + grad_direct + electron_grad
    return (single_out, pair_out, grad_single, grad_pair)


def solution(mesh):
    placed = (
        P("walk", ("row", "col"), None),
        P("walk", "row", "col", None),
        P(),
        P(),
        P(),
        P(),
        P(),
        P(),
        P("walk", ("row", "col"), None),
        P("walk", "row", "col", None),
    )
    return jax.shard_map(
        body,
        mesh=mesh,
        in_specs=placed,
        out_specs=(
            P("walk", ("row", "col"), None),
            P("walk", "row", "col", None),
            P("walk", ("row", "col"), None),
            P("walk", "row", "col", None),
        ),
        check_vma=False,
    )
```

```python
import jax
import jax.numpy as jnp
from jax import lax
from jax.experimental import pallas as pl
from jax.experimental.pallas import tpu as pltpu
from jax.sharding import PartitionSpec as P

def pair_kernel(pair_ref, dpair_ref, msg_ref, wp_ref, wpt_ref, b_ref, mask_ref, aup_ref, adn_ref,
                *rest):
    out_ref, grad_ref, col_ref = rest[-3:]
    i = pl.program_id(1)
    ti, bc, dp = pair_ref.shape[1:]
    x = pair_ref[0]
    pre = jnp.dot(x.reshape(ti * bc, dp), wp_ref[...], preferred_element_type=jnp.float32)
    pre = pre.reshape(ti, bc, dp) + msg_ref[0][None] + b_ref[...][None]
    act = jnp.tanh(pre)
    out_ref[0] = (x.astype(jnp.float32) + act).astype(out_ref.dtype)
    d = dpair_ref[0].astype(jnp.float32)
    delta = (d * (1.0 - act * act)).astype(jnp.bfloat16)
    back = jnp.dot(delta.reshape(ti * bc, dp), wpt_ref[...], preferred_element_type=jnp.float32)
    spread = jnp.where(mask_ref[...][None] > 0.5, aup_ref[0][:, None, :], adn_ref[0][:, None, :])
    grad_ref[0] = (d + back.reshape(ti, bc, dp) + spread).astype(grad_ref.dtype)
    part = jnp.sum(delta.astype(jnp.float32), axis=0)

    @pl.when(i == 0)
    def _():
        col_ref[0] = part

    @pl.when(i > 0)
    def _():
        col_ref[0] = col_ref[0] + part


def pair_pass(pair, d_pair, message_b, w_pair, b_pair, up_mask, a_up, a_down, first, prev=None):
    w, br, bc, dp = pair.shape
    group = message_b.shape[0]
    ti = max(1, min(br, 8192 // bc))
    grid = (group, br // ti)
    blk = pl.BlockSpec((1, ti, bc, dp), lambda a, i: (a + first, i, 0, 0))
    whole2 = lambda shape: pl.BlockSpec(shape, lambda a, i: (0, 0))
    per_w = pl.BlockSpec((1, bc, dp), lambda a, i: (a, 0, 0))
    rows = pl.BlockSpec((1, ti, dp), lambda a, i: (a, i, 0))
    in_specs = [blk, blk, per_w, whole2((dp, dp)), whole2((dp, dp)), whole2((1, dp)),
                whole2((bc, dp)), rows, rows]
    args = [pair, d_pair, message_b, w_pair, w_pair.T, b_pair.reshape(1, dp), up_mask, a_up, a_down]
    aliases = {}
    if prev is not None:
        in_specs += [pl.BlockSpec(memory_space=pl.ANY), pl.BlockSpec(memory_space=pl.ANY)]
        aliases = {len(args): 0, len(args) + 1: 1}
        args += list(prev)
    return pl.pallas_call(
        pair_kernel,
        grid=grid,
        in_specs=in_specs,
        out_specs=[blk, blk, per_w],
        out_shape=[jax.ShapeDtypeStruct(pair.shape, jnp.bfloat16),
                   jax.ShapeDtypeStruct(pair.shape, jnp.bfloat16),
                   jax.ShapeDtypeStruct((group, bc, dp), jnp.float32)],
        input_output_aliases=aliases,
        cost_estimate=pl.CostEstimate(
            flops=4 * group * br * bc * dp * dp,
            transcendentals=group * br * bc * dp,
            bytes_accessed=8 * group * br * bc * dp,
        ),
        compiler_params=pltpu.CompilerParams(dimension_semantics=("arbitrary", "arbitrary")),
    )(*args)


highest = lax.Precision.HIGHEST


def roll_pieces(pieces, shift):
    n = pieces.shape[0]
    doubled = jnp.concatenate([pieces, pieces], axis=0)
    return lax.dynamic_slice_in_dim(doubled, (n - shift) % n, n, 0)


def body(one_elec, pair, spins, w_single, b_single, w_pair, w_msg, b_pair, d_single, d_pair):
    walkers, block_rows, block_cols, width_pair = pair.shape
    own_rows = one_elec.shape[1]
    width_single = one_elec.shape[2]
    electrons = spins.shape[0]
    rows = electrons // block_rows
    cols = electrons // block_cols
    assert rows == cols
    pair_down = float(electrons) ** (-0.75)
    pair_boost = float(electrons) ** 0.75
    row_index = lax.axis_index("row")
    col_index = lax.axis_index("col")
    spin_up = spins.astype(jnp.float32)
    spin_down = 1.0 - spin_up
    count_up = jnp.sum(spin_up)
    count_down = jnp.sum(spin_down)
    counts = jnp.stack([count_up, count_down])
    spin_table = jnp.stack([spin_up, spin_down], axis=1)
    col_start = col_index * block_cols
    own_start = (row_index * cols + col_index) * own_rows
    col_table = lax.dynamic_slice_in_dim(spin_table, col_start, block_cols, 0)
    own_table = lax.dynamic_slice_in_dim(spin_table, own_start, own_rows, 0)

    both = ("row", "col")
    pieces = []
    for s in range(rows):
        perm = [(a * cols + b, ((b - s) % rows) * cols + a) for a in range(rows) for b in range(cols)]
        pieces.append(lax.ppermute(one_elec, both, perm))
    col_single = roll_pieces(jnp.stack(pieces), row_index)
    col_single = jnp.moveaxis(col_single, 0, 1).reshape(walkers, block_cols, width_single)

    col_spin_sums = jnp.einsum(
        "wjd,js->wsd", col_single, col_table.astype(jnp.bfloat16), preferred_element_type=jnp.float32
    )
    partial_value = jnp.einsum(
        "wijd,js->wisd", pair, col_table.astype(jnp.bfloat16), preferred_element_type=jnp.float32
    )
    sub_value = partial_value.reshape(walkers, cols, own_rows, 2, width_pair)
    own_sum = lax.dynamic_index_in_dim(sub_value, col_index, 1, keepdims=False)
    spin_sums = col_spin_sums
    spin_hi = col_spin_sums.astype(jnp.bfloat16)
    spin_lo = (col_spin_sums - spin_hi.astype(jnp.float32)).astype(jnp.bfloat16)
    split = own_rows * 2 * width_pair
    spin_size = 2 * width_single
    for s in range(1, cols):
        dest = col_index ^ s
        sent = lax.dynamic_index_in_dim(sub_value, dest, 1, keepdims=False)
        payload = jnp.concatenate(
            [
                sent.astype(jnp.bfloat16).reshape(walkers, -1),
                spin_hi.reshape(walkers, -1),
                spin_lo.reshape(walkers, -1),
            ],
            axis=1,
        )
        got = lax.ppermute(payload, "col", [(b, b ^ s) for b in range(cols)])
        own_sum = own_sum + got[:, :split].astype(jnp.float32).reshape(own_sum.shape)
        got_hi = got[:, split : split + spin_size].astype(jnp.float32)
        got_lo = got[:, split + spin_size :].astype(jnp.float32)
        spin_sums = spin_sums + (got_hi + got_lo).reshape(spin_sums.shape)

    spin_means = spin_sums / counts[None, :, None]
    pair_means = own_sum / counts[None, None, :, None]
    single_wide = one_elec.astype(jnp.float32)
    features = jnp.concatenate(
        [
            single_wide,
            jnp.broadcast_to(spin_means[:, None, 0, :], (walkers, own_rows, width_single)),
            jnp.broadcast_to(spin_means[:, None, 1, :], (walkers, own_rows, width_single)),
            pair_means[:, :, 0, :],
            pair_means[:, :, 1, :],
        ],
        axis=2,
    ).astype(jnp.bfloat16)
    single_act = jnp.tanh(
        jnp.einsum("wif,fd->wid", features, w_single, preferred_element_type=jnp.float32) + b_single
    )
    single_out = (single_wide + single_act).astype(jnp.bfloat16)
    grad_pre = (d_single.astype(jnp.float32) * (1.0 - single_act * single_act)).astype(jnp.bfloat16)
    feature_grad = jnp.einsum("wid,fd->wif", grad_pre, w_single, preferred_element_type=jnp.float32)
    grad_direct = feature_grad[:, :, :width_single]
    grad_means = feature_grad[:, :, width_single : 3 * width_single].reshape(
        walkers, own_rows, 2, width_single
    )
    grad_pair_means = feature_grad[:, :, 3 * width_single :].reshape(
        walkers, own_rows, 2, width_pair
    )
    mean_sums = jnp.sum(grad_means, axis=1)

    mean_hi = mean_sums.astype(jnp.bfloat16)
    mean_lo = (mean_sums - mean_hi.astype(jnp.float32)).astype(jnp.bfloat16)
    payload = jnp.concatenate(
        [
            grad_pair_means.astype(jnp.bfloat16).reshape(walkers, -1),
            mean_hi.reshape(walkers, -1),
            mean_lo.reshape(walkers, -1),
        ],
        axis=1,
    )
    split = own_rows * 2 * width_pair
    mean_size = 2 * width_single
    gathered = [grad_pair_means.astype(jnp.bfloat16).astype(jnp.float32)] + [None] * (cols - 1)
    mean_part = mean_sums
    for s in range(1, cols):
        got = lax.ppermute(payload, "col", [(b, b ^ s) for b in range(cols)])
        gathered[s] = got[:, :split].astype(jnp.float32).reshape(grad_pair_means.shape)
        got_hi = got[:, split : split + mean_size].astype(jnp.float32)
        got_lo = got[:, split + mean_size :].astype(jnp.float32)
        mean_part = mean_part + (got_hi + got_lo).reshape(mean_sums.shape)
    gathered = jnp.stack(gathered)
    order = jnp.arange(cols) ^ col_index
    row_pair_grads = jnp.take(gathered, order, axis=0)
    row_pair_grads = jnp.moveaxis(row_pair_grads, 0, 1).reshape(walkers, block_rows, 2, width_pair)

    message = jnp.einsum("wjd,de->wje", col_single, w_msg, preferred_element_type=jnp.float32)
    a_up = pair_boost * (row_pair_grads[:, :, 0, :] / count_up)
    a_down = pair_boost * (row_pair_grads[:, :, 1, :] / count_down)
    up_mask = jnp.broadcast_to(col_table[:, :1], (block_cols, width_pair))
    pair_out, grad_pair, column_sum = pair_pass(
        pair, d_pair, message, w_pair, b_pair, up_mask, a_up, a_down, 0
    )

    sub_cols = column_sum.reshape(walkers, rows, own_rows, width_pair)
    mean_hi = mean_part.astype(jnp.bfloat16)
    mean_lo = (mean_part - mean_hi.astype(jnp.float32)).astype(jnp.bfloat16)
    split = own_rows * width_pair
    mean_size = 2 * width_single
    own_cols = None
    mean_total = None
    for s in range(rows):
        sent = lax.dynamic_index_in_dim(sub_cols, (row_index + s) % rows, 1, keepdims=False)
        payload = jnp.concatenate(
            [
                sent.astype(jnp.bfloat16).reshape(walkers, -1),
                mean_hi.reshape(walkers, -1),
                mean_lo.reshape(walkers, -1),
            ],
            axis=1,
        )
        perm = [(a * cols + b, b * cols + (a + s) % rows) for a in range(rows) for b in range(cols)]
        got = lax.ppermute(payload, both, perm)
        got_cols = got[:, :split].astype(jnp.float32).reshape(walkers, own_rows, width_pair)
        got_hi = got[:, split : split + mean_size].astype(jnp.float32)
        got_lo = got[:, split + mean_size :].astype(jnp.float32)
        got_mean = (got_hi + got_lo).reshape(mean_part.shape)
        own_cols = got_cols if own_cols is None else own_cols + got_cols
        mean_total = got_mean if mean_total is None else mean_total + got_mean

    own_message = pair_down * jnp.einsum(
        "wje,de->wjd", own_cols, w_msg.astype(jnp.float32), precision=highest
    )
    own_up = own_table[:, 0]
    own_down = own_table[:, 1]
    electron_grad = (
        own_up[None, :, None] * (mean_total[:, 0, :] / count_up)[:, None, :]
        + own_down[None, :, None] * (mean_total[:, 1, :] / count_down)[:, None, :]
        + own_message
    )
    grad_single = d_single.astype(jnp.float32) + grad_direct + electron_grad
    return (single_out, pair_out, grad_single, grad_pair)


def solution(mesh):
    placed = (
        P("walk", ("row", "col"), None),
        P("walk", "row", "col", None),
        P(),
        P(),
        P(),
        P(),
        P(),
        P(),
        P("walk", ("row", "col"), None),
        P("walk", "row", "col", None),
    )
    return jax.shard_map(
        body,
        mesh=mesh,
        in_specs=placed,
        out_specs=(
            P("walk", ("row", "col"), None),
            P("walk", "row", "col", None),
            P("walk", ("row", "col"), None),
            P("walk", "row", "col", None),
        ),
        check_vma=False,
    )
```

```python
import jax
import jax.numpy as jnp
from jax import lax
from jax.experimental import pallas as pl
from jax.experimental.pallas import tpu as pltpu
from jax.sharding import PartitionSpec as P

def pair_kernel(pair_ref, dpair_ref, msg_ref, wp_ref, wpt_ref, b_ref, mask_ref, aup_ref, adn_ref,
                *rest):
    out_ref, grad_ref, col_ref = rest[-3:]
    i = pl.program_id(1)
    ti, bc, dp = pair_ref.shape[1:]
    x = pair_ref[0]
    pre = jnp.dot(x.reshape(ti * bc, dp), wp_ref[...], preferred_element_type=jnp.float32)
    pre = pre.reshape(ti, bc, dp) + msg_ref[0][None] + b_ref[...][None]
    act = jnp.tanh(pre)
    out_ref[0] = (x.astype(jnp.float32) + act).astype(out_ref.dtype)
    d = dpair_ref[0].astype(jnp.float32)
    delta = (d * (1.0 - act * act)).astype(jnp.bfloat16)
    back = jnp.dot(delta.reshape(ti * bc, dp), wpt_ref[...], preferred_element_type=jnp.float32)
    spread = jnp.where(mask_ref[...][None] > 0.5, aup_ref[0][:, None, :], adn_ref[0][:, None, :])
    grad_ref[0] = (d + back.reshape(ti, bc, dp) + spread).astype(grad_ref.dtype)
    part = jnp.sum(delta.astype(jnp.float32), axis=0)

    @pl.when(i == 0)
    def _():
        col_ref[0] = part

    @pl.when(i > 0)
    def _():
        col_ref[0] = col_ref[0] + part


def pair_pass(pair, d_pair, message_b, w_pair, b_pair, up_mask, a_up, a_down, first, prev=None):
    w, br, bc, dp = pair.shape
    group = message_b.shape[0]
    ti = max(1, min(br, 8192 // bc))
    grid = (group, br // ti)
    blk = pl.BlockSpec((1, ti, bc, dp), lambda a, i: (a + first, i, 0, 0))
    whole2 = lambda shape: pl.BlockSpec(shape, lambda a, i: (0, 0))
    per_w = pl.BlockSpec((1, bc, dp), lambda a, i: (a, 0, 0))
    rows = pl.BlockSpec((1, ti, dp), lambda a, i: (a, i, 0))
    in_specs = [blk, blk, per_w, whole2((dp, dp)), whole2((dp, dp)), whole2((1, dp)),
                whole2((bc, dp)), rows, rows]
    args = [pair, d_pair, message_b, w_pair, w_pair.T, b_pair.reshape(1, dp), up_mask, a_up, a_down]
    aliases = {}
    if prev is not None:
        in_specs += [pl.BlockSpec(memory_space=pl.ANY), pl.BlockSpec(memory_space=pl.ANY)]
        aliases = {len(args): 0, len(args) + 1: 1}
        args += list(prev)
    return pl.pallas_call(
        pair_kernel,
        grid=grid,
        in_specs=in_specs,
        out_specs=[blk, blk, per_w],
        out_shape=[jax.ShapeDtypeStruct(pair.shape, jnp.bfloat16),
                   jax.ShapeDtypeStruct(pair.shape, jnp.bfloat16),
                   jax.ShapeDtypeStruct((group, bc, dp), jnp.float32)],
        input_output_aliases=aliases,
        cost_estimate=pl.CostEstimate(
            flops=4 * group * br * bc * dp * dp,
            transcendentals=group * br * bc * dp,
            bytes_accessed=8 * group * br * bc * dp,
        ),
        compiler_params=pltpu.CompilerParams(dimension_semantics=("arbitrary", "arbitrary")),
    )(*args)


highest = lax.Precision.HIGHEST


def roll_pieces(pieces, shift):
    n = pieces.shape[0]
    doubled = jnp.concatenate([pieces, pieces], axis=0)
    return lax.dynamic_slice_in_dim(doubled, (n - shift) % n, n, 0)


def body(one_elec, pair, spins, w_single, b_single, w_pair, w_msg, b_pair, d_single, d_pair):
    walkers, block_rows, block_cols, width_pair = pair.shape
    own_rows = one_elec.shape[1]
    width_single = one_elec.shape[2]
    electrons = spins.shape[0]
    rows = electrons // block_rows
    cols = electrons // block_cols
    assert rows == cols
    pair_down = float(electrons) ** (-0.75)
    pair_boost = float(electrons) ** 0.75
    row_index = lax.axis_index("row")
    col_index = lax.axis_index("col")
    spin_up = spins.astype(jnp.float32)
    spin_down = 1.0 - spin_up
    count_up = jnp.sum(spin_up)
    count_down = jnp.sum(spin_down)
    counts = jnp.stack([count_up, count_down])
    spin_table = jnp.stack([spin_up, spin_down], axis=1)
    col_start = col_index * block_cols
    own_start = (row_index * cols + col_index) * own_rows
    col_table = lax.dynamic_slice_in_dim(spin_table, col_start, block_cols, 0)
    own_table = lax.dynamic_slice_in_dim(spin_table, own_start, own_rows, 0)

    both = ("row", "col")
    pieces = [one_elec] + [None] * (cols - 1)
    for s in range(1, cols):
        pieces[s] = lax.ppermute(one_elec, "col", [(b, b ^ s) for b in range(cols)])
    order = jnp.arange(cols) ^ col_index
    row_single = jnp.take(jnp.stack(pieces), order, axis=0)
    row_single = jnp.moveaxis(row_single, 0, 1).reshape(walkers, block_rows, width_single)
    col_single = lax.ppermute(
        row_single, both, [(a * cols + b, b * cols + a) for a in range(rows) for b in range(cols)]
    )

    col_spin_sums = jnp.einsum(
        "wjd,js->wsd", col_single, col_table.astype(jnp.bfloat16), preferred_element_type=jnp.float32
    )
    partial_value = jnp.einsum(
        "wijd,js->wisd", pair, col_table.astype(jnp.bfloat16), preferred_element_type=jnp.float32
    )
    sub_value = partial_value.reshape(walkers, cols, own_rows, 2, width_pair)
    own_sum = lax.dynamic_index_in_dim(sub_value, col_index, 1, keepdims=False)
    spin_sums = col_spin_sums
    spin_hi = col_spin_sums.astype(jnp.bfloat16)
    spin_lo = (col_spin_sums - spin_hi.astype(jnp.float32)).astype(jnp.bfloat16)
    split = own_rows * 2 * width_pair
    spin_size = 2 * width_single
    for s in range(1, cols):
        dest = col_index ^ s
        sent = lax.dynamic_index_in_dim(sub_value, dest, 1, keepdims=False)
        payload = jnp.concatenate(
            [
                sent.astype(jnp.bfloat16).reshape(walkers, -1),
                spin_hi.reshape(walkers, -1),
                spin_lo.reshape(walkers, -1),
            ],
            axis=1,
        )
        got = lax.ppermute(payload, "col", [(b, b ^ s) for b in range(cols)])
        own_sum = own_sum + got[:, :split].astype(jnp.float32).reshape(own_sum.shape)
        got_hi = got[:, split : split + spin_size].astype(jnp.float32)
        got_lo = got[:, split + spin_size :].astype(jnp.float32)
        spin_sums = spin_sums + (got_hi + got_lo).reshape(spin_sums.shape)

    spin_means = spin_sums / counts[None, :, None]
    pair_means = own_sum / counts[None, None, :, None]
    single_wide = one_elec.astype(jnp.float32)
    features = jnp.concatenate(
        [
            single_wide,
            jnp.broadcast_to(spin_means[:, None, 0, :], (walkers, own_rows, width_single)),
            jnp.broadcast_to(spin_means[:, None, 1, :], (walkers, own_rows, width_single)),
            pair_means[:, :, 0, :],
            pair_means[:, :, 1, :],
        ],
        axis=2,
    ).astype(jnp.bfloat16)
    single_act = jnp.tanh(
        jnp.einsum("wif,fd->wid", features, w_single, preferred_element_type=jnp.float32) + b_single
    )
    single_out = (single_wide + single_act).astype(jnp.bfloat16)
    grad_pre = (d_single.astype(jnp.float32) * (1.0 - single_act * single_act)).astype(jnp.bfloat16)
    feature_grad = jnp.einsum("wid,fd->wif", grad_pre, w_single, preferred_element_type=jnp.float32)
    grad_direct = feature_grad[:, :, :width_single]
    grad_means = feature_grad[:, :, width_single : 3 * width_single].reshape(
        walkers, own_rows, 2, width_single
    )
    grad_pair_means = feature_grad[:, :, 3 * width_single :].reshape(
        walkers, own_rows, 2, width_pair
    )
    mean_sums = jnp.sum(grad_means, axis=1)

    mean_hi = mean_sums.astype(jnp.bfloat16)
    mean_lo = (mean_sums - mean_hi.astype(jnp.float32)).astype(jnp.bfloat16)
    payload = jnp.concatenate(
        [
            grad_pair_means.astype(jnp.bfloat16).reshape(walkers, -1),
            mean_hi.reshape(walkers, -1),
            mean_lo.reshape(walkers, -1),
        ],
        axis=1,
    )
    split = own_rows * 2 * width_pair
    mean_size = 2 * width_single
    gathered = [grad_pair_means.astype(jnp.bfloat16).astype(jnp.float32)] + [None] * (cols - 1)
    mean_part = mean_sums
    for s in range(1, cols):
        got = lax.ppermute(payload, "col", [(b, b ^ s) for b in range(cols)])
        gathered[s] = got[:, :split].astype(jnp.float32).reshape(grad_pair_means.shape)
        got_hi = got[:, split : split + mean_size].astype(jnp.float32)
        got_lo = got[:, split + mean_size :].astype(jnp.float32)
        mean_part = mean_part + (got_hi + got_lo).reshape(mean_sums.shape)
    gathered = jnp.stack(gathered)
    order = jnp.arange(cols) ^ col_index
    row_pair_grads = jnp.take(gathered, order, axis=0)
    row_pair_grads = jnp.moveaxis(row_pair_grads, 0, 1).reshape(walkers, block_rows, 2, width_pair)

    message = jnp.einsum("wjd,de->wje", col_single, w_msg, preferred_element_type=jnp.float32)
    a_up = pair_boost * (row_pair_grads[:, :, 0, :] / count_up)
    a_down = pair_boost * (row_pair_grads[:, :, 1, :] / count_down)
    up_mask = jnp.broadcast_to(col_table[:, :1], (block_cols, width_pair))
    pair_out, grad_pair, column_sum = pair_pass(
        pair, d_pair, message, w_pair, b_pair, up_mask, a_up, a_down, 0
    )

    sub_cols = column_sum.reshape(walkers, rows, own_rows, width_pair)
    mean_hi = mean_part.astype(jnp.bfloat16)
    mean_lo = (mean_part - mean_hi.astype(jnp.float32)).astype(jnp.bfloat16)
    split = own_rows * width_pair
    mean_size = 2 * width_single
    own_cols = None
    mean_total = None
    for s in range(rows):
        sent = lax.dynamic_index_in_dim(sub_cols, (row_index + s) % rows, 1, keepdims=False)
        payload = jnp.concatenate(
            [
                sent.astype(jnp.bfloat16).reshape(walkers, -1),
                mean_hi.reshape(walkers, -1),
                mean_lo.reshape(walkers, -1),
            ],
            axis=1,
        )
        perm = [(a * cols + b, b * cols + (a + s) % rows) for a in range(rows) for b in range(cols)]
        got = lax.ppermute(payload, both, perm)
        got_cols = got[:, :split].astype(jnp.float32).reshape(walkers, own_rows, width_pair)
        got_hi = got[:, split : split + mean_size].astype(jnp.float32)
        got_lo = got[:, split + mean_size :].astype(jnp.float32)
        got_mean = (got_hi + got_lo).reshape(mean_part.shape)
        own_cols = got_cols if own_cols is None else own_cols + got_cols
        mean_total = got_mean if mean_total is None else mean_total + got_mean

    own_message = pair_down * jnp.einsum(
        "wje,de->wjd", own_cols, w_msg.astype(jnp.float32), precision=highest
    )
    own_up = own_table[:, 0]
    own_down = own_table[:, 1]
    electron_grad = (
        own_up[None, :, None] * (mean_total[:, 0, :] / count_up)[:, None, :]
        + own_down[None, :, None] * (mean_total[:, 1, :] / count_down)[:, None, :]
        + own_message
    )
    grad_single = d_single.astype(jnp.float32) + grad_direct + electron_grad
    return (single_out, pair_out, grad_single, grad_pair)


def solution(mesh):
    placed = (
        P("walk", ("row", "col"), None),
        P("walk", "row", "col", None),
        P(),
        P(),
        P(),
        P(),
        P(),
        P(),
        P("walk", ("row", "col"), None),
        P("walk", "row", "col", None),
    )
    return jax.shard_map(
        body,
        mesh=mesh,
        in_specs=placed,
        out_specs=(
            P("walk", ("row", "col"), None),
            P("walk", "row", "col", None),
            P("walk", ("row", "col"), None),
            P("walk", "row", "col", None),
        ),
        check_vma=False,
    )
```

```python
import jax
import jax.numpy as jnp
from jax import lax
from jax.experimental import pallas as pl
from jax.experimental.pallas import tpu as pltpu
from jax.sharding import PartitionSpec as P

def pair_kernel(pair_ref, dpair_ref, msg_ref, wp_ref, wpt_ref, b_ref, mask_ref, aup_ref, adn_ref,
                *rest):
    out_ref, grad_ref, col_ref = rest[-3:]
    i = pl.program_id(1)
    ti, bc, dp = pair_ref.shape[1:]
    x = pair_ref[0]
    pre = jnp.dot(x.reshape(ti * bc, dp), wp_ref[...], preferred_element_type=jnp.float32)
    pre = pre.reshape(ti, bc, dp) + msg_ref[0][None] + b_ref[...][None]
    act = jnp.tanh(pre)
    out_ref[0] = (x.astype(jnp.float32) + act).astype(out_ref.dtype)
    d = dpair_ref[0].astype(jnp.float32)
    delta = (d * (1.0 - act * act)).astype(jnp.bfloat16)
    back = jnp.dot(delta.reshape(ti * bc, dp), wpt_ref[...], preferred_element_type=jnp.float32)
    spread = jnp.where(mask_ref[...][None] > 0.5, aup_ref[0][:, None, :], adn_ref[0][:, None, :])
    grad_ref[0] = (d + back.reshape(ti, bc, dp) + spread).astype(grad_ref.dtype)
    part = jnp.sum(delta.astype(jnp.float32), axis=0)

    @pl.when(i == 0)
    def _():
        col_ref[0] = part

    @pl.when(i > 0)
    def _():
        col_ref[0] = col_ref[0] + part


def pair_pass(pair, d_pair, message_b, w_pair, b_pair, up_mask, a_up, a_down, first, prev=None):
    w, br, bc, dp = pair.shape
    group = message_b.shape[0]
    ti = max(1, min(br, 8192 // bc))
    grid = (group, br // ti)
    blk = pl.BlockSpec((1, ti, bc, dp), lambda a, i: (a + first, i, 0, 0))
    whole2 = lambda shape: pl.BlockSpec(shape, lambda a, i: (0, 0))
    per_w = pl.BlockSpec((1, bc, dp), lambda a, i: (a, 0, 0))
    rows = pl.BlockSpec((1, ti, dp), lambda a, i: (a, i, 0))
    in_specs = [blk, blk, per_w, whole2((dp, dp)), whole2((dp, dp)), whole2((1, dp)),
                whole2((bc, dp)), rows, rows]
    args = [pair, d_pair, message_b, w_pair, w_pair.T, b_pair.reshape(1, dp), up_mask, a_up, a_down]
    aliases = {}
    if prev is not None:
        in_specs += [pl.BlockSpec(memory_space=pl.ANY), pl.BlockSpec(memory_space=pl.ANY)]
        aliases = {len(args): 0, len(args) + 1: 1}
        args += list(prev)
    return pl.pallas_call(
        pair_kernel,
        grid=grid,
        in_specs=in_specs,
        out_specs=[blk, blk, per_w],
        out_shape=[jax.ShapeDtypeStruct(pair.shape, jnp.bfloat16),
                   jax.ShapeDtypeStruct(pair.shape, jnp.bfloat16),
                   jax.ShapeDtypeStruct((group, bc, dp), jnp.float32)],
        input_output_aliases=aliases,
        cost_estimate=pl.CostEstimate(
            flops=4 * group * br * bc * dp * dp,
            transcendentals=group * br * bc * dp,
            bytes_accessed=8 * group * br * bc * dp,
        ),
        compiler_params=pltpu.CompilerParams(dimension_semantics=("arbitrary", "arbitrary")),
    )(*args)


highest = lax.Precision.HIGHEST


def roll_pieces(pieces, shift):
    n = pieces.shape[0]
    doubled = jnp.concatenate([pieces, pieces], axis=0)
    return lax.dynamic_slice_in_dim(doubled, (n - shift) % n, n, 0)


def body(one_elec, pair, spins, w_single, b_single, w_pair, w_msg, b_pair, d_single, d_pair):
    walkers, block_rows, block_cols, width_pair = pair.shape
    own_rows = one_elec.shape[1]
    width_single = one_elec.shape[2]
    electrons = spins.shape[0]
    rows = electrons // block_rows
    cols = electrons // block_cols
    assert rows == cols
    pair_down = float(electrons) ** (-0.75)
    pair_boost = float(electrons) ** 0.75
    row_index = lax.axis_index("row")
    col_index = lax.axis_index("col")
    spin_up = spins.astype(jnp.float32)
    spin_down = 1.0 - spin_up
    count_up = jnp.sum(spin_up)
    count_down = jnp.sum(spin_down)
    counts = jnp.stack([count_up, count_down])
    spin_table = jnp.stack([spin_up, spin_down], axis=1)
    col_start = col_index * block_cols
    own_start = (row_index * cols + col_index) * own_rows
    col_table = lax.dynamic_slice_in_dim(spin_table, col_start, block_cols, 0)
    own_table = lax.dynamic_slice_in_dim(spin_table, own_start, own_rows, 0)

    both = ("row", "col")
    pieces = []
    for s in range(rows):
        perm = [(a * cols + b, ((b - s) % rows) * cols + a) for a in range(rows) for b in range(cols)]
        pieces.append(lax.ppermute(one_elec, both, perm))
    col_single = roll_pieces(jnp.stack(pieces), row_index)
    col_single = jnp.moveaxis(col_single, 0, 1).reshape(walkers, block_cols, width_single)

    col_spin_sums = jnp.einsum(
        "wjd,js->wsd", col_single, col_table.astype(jnp.bfloat16), preferred_element_type=jnp.float32
    )
    partial_value = jnp.einsum(
        "wijd,js->wisd", pair, col_table.astype(jnp.bfloat16), preferred_element_type=jnp.float32
    )
    sub_value = partial_value.reshape(walkers, cols, own_rows, 2, width_pair)
    own_sum = lax.dynamic_index_in_dim(sub_value, col_index, 1, keepdims=False)
    spin_sums = col_spin_sums
    spin_hi = col_spin_sums.astype(jnp.bfloat16)
    spin_lo = (col_spin_sums - spin_hi.astype(jnp.float32)).astype(jnp.bfloat16)
    split = own_rows * 2 * width_pair
    spin_size = 2 * width_single
    for s in range(1, cols):
        dest = col_index ^ s
        sent = lax.dynamic_index_in_dim(sub_value, dest, 1, keepdims=False)
        payload = jnp.concatenate(
            [
                sent.astype(jnp.bfloat16).reshape(walkers, -1),
                spin_hi.reshape(walkers, -1),
                spin_lo.reshape(walkers, -1),
            ],
            axis=1,
        )
        got = lax.ppermute(payload, "col", [(b, b ^ s) for b in range(cols)])
        own_sum = own_sum + got[:, :split].astype(jnp.float32).reshape(own_sum.shape)
        got_hi = got[:, split : split + spin_size].astype(jnp.float32)
        got_lo = got[:, split + spin_size :].astype(jnp.float32)
        spin_sums = spin_sums + (got_hi + got_lo).reshape(spin_sums.shape)

    spin_means = spin_sums / counts[None, :, None]
    pair_means = own_sum / counts[None, None, :, None]
    single_wide = one_elec.astype(jnp.float32)
    features = jnp.concatenate(
        [
            single_wide,
            jnp.broadcast_to(spin_means[:, None, 0, :], (walkers, own_rows, width_single)),
            jnp.broadcast_to(spin_means[:, None, 1, :], (walkers, own_rows, width_single)),
            pair_means[:, :, 0, :],
            pair_means[:, :, 1, :],
        ],
        axis=2,
    ).astype(jnp.bfloat16)
    single_act = jnp.tanh(
        jnp.einsum("wif,fd->wid", features, w_single, preferred_element_type=jnp.float32) + b_single
    )
    single_out = (single_wide + single_act).astype(jnp.bfloat16)
    grad_pre = (d_single.astype(jnp.float32) * (1.0 - single_act * single_act)).astype(jnp.bfloat16)
    feature_grad = jnp.einsum("wid,fd->wif", grad_pre, w_single, preferred_element_type=jnp.float32)
    grad_direct = feature_grad[:, :, :width_single]
    grad_means = feature_grad[:, :, width_single : 3 * width_single].reshape(
        walkers, own_rows, 2, width_single
    )
    grad_pair_means = feature_grad[:, :, 3 * width_single :].reshape(
        walkers, own_rows, 2, width_pair
    )
    mean_sums = jnp.sum(grad_means, axis=1)

    mean_hi = mean_sums.astype(jnp.bfloat16)
    mean_lo = (mean_sums - mean_hi.astype(jnp.float32)).astype(jnp.bfloat16)
    payload = jnp.concatenate(
        [
            grad_pair_means.astype(jnp.bfloat16).reshape(walkers, -1),
            mean_hi.reshape(walkers, -1),
            mean_lo.reshape(walkers, -1),
        ],
        axis=1,
    )
    split = own_rows * 2 * width_pair
    mean_size = 2 * width_single
    gathered = [grad_pair_means.astype(jnp.bfloat16).astype(jnp.float32)] + [None] * (cols - 1)
    mean_part = mean_sums
    for s in range(1, cols):
        got = lax.ppermute(payload, "col", [(b, b ^ s) for b in range(cols)])
        gathered[s] = got[:, :split].astype(jnp.float32).reshape(grad_pair_means.shape)
        got_hi = got[:, split : split + mean_size].astype(jnp.float32)
        got_lo = got[:, split + mean_size :].astype(jnp.float32)
        mean_part = mean_part + (got_hi + got_lo).reshape(mean_sums.shape)
    gathered = jnp.stack(gathered)
    order = jnp.arange(cols) ^ col_index
    row_pair_grads = jnp.take(gathered, order, axis=0)
    row_pair_grads = jnp.moveaxis(row_pair_grads, 0, 1).reshape(walkers, block_rows, 2, width_pair)

    message = jnp.einsum("wjd,de->wje", col_single, w_msg, preferred_element_type=jnp.float32)
    a_up = pair_boost * (row_pair_grads[:, :, 0, :] / count_up)
    a_down = pair_boost * (row_pair_grads[:, :, 1, :] / count_down)
    up_mask = jnp.broadcast_to(col_table[:, :1], (block_cols, width_pair))
    pair_out, grad_pair, column_sum = pair_pass(
        pair, d_pair, message, w_pair, b_pair, up_mask, a_up, a_down, 0
    )

    sub_cols = column_sum.reshape(walkers, rows, own_rows, width_pair)
    mean_hi = mean_part.astype(jnp.bfloat16)
    mean_lo = (mean_part - mean_hi.astype(jnp.float32)).astype(jnp.bfloat16)
    split = own_rows * width_pair
    mean_size = 2 * width_single
    block_sum = lax.dynamic_index_in_dim(sub_cols, row_index, 1, keepdims=False)
    mean_total = mean_part
    for s in range(1, rows):
        sent = lax.dynamic_index_in_dim(sub_cols, row_index ^ s, 1, keepdims=False)
        payload = jnp.concatenate(
            [
                sent.astype(jnp.bfloat16).reshape(walkers, -1),
                mean_hi.reshape(walkers, -1),
                mean_lo.reshape(walkers, -1),
            ],
            axis=1,
        )
        got = lax.ppermute(payload, "row", [(a, a ^ s) for a in range(rows)])
        block_sum = block_sum + got[:, :split].astype(jnp.float32).reshape(block_sum.shape)
        got_hi = got[:, split : split + mean_size].astype(jnp.float32)
        got_lo = got[:, split + mean_size :].astype(jnp.float32)
        mean_total = mean_total + (got_hi + got_lo).reshape(mean_part.shape)
    sum_hi = block_sum.astype(jnp.bfloat16)
    sum_lo = (block_sum - sum_hi.astype(jnp.float32)).astype(jnp.bfloat16)
    got = lax.ppermute(
        jnp.stack([sum_hi, sum_lo]),
        both,
        [(a * cols + b, b * cols + a) for a in range(rows) for b in range(cols)],
    )
    own_cols = got[0].astype(jnp.float32) + got[1].astype(jnp.float32)

    own_message = pair_down * jnp.einsum(
        "wje,de->wjd", own_cols, w_msg.astype(jnp.float32), precision=highest
    )
    own_up = own_table[:, 0]
    own_down = own_table[:, 1]
    electron_grad = (
        own_up[None, :, None] * (mean_total[:, 0, :] / count_up)[:, None, :]
        + own_down[None, :, None] * (mean_total[:, 1, :] / count_down)[:, None, :]
        + own_message
    )
    grad_single = d_single.astype(jnp.float32) + grad_direct + electron_grad
    return (single_out, pair_out, grad_single, grad_pair)


def solution(mesh):
    placed = (
        P("walk", ("row", "col"), None),
        P("walk", "row", "col", None),
        P(),
        P(),
        P(),
        P(),
        P(),
        P(),
        P("walk", ("row", "col"), None),
        P("walk", "row", "col", None),
    )
    return jax.shard_map(
        body,
        mesh=mesh,
        in_specs=placed,
        out_specs=(
            P("walk", ("row", "col"), None),
            P("walk", "row", "col", None),
            P("walk", ("row", "col"), None),
            P("walk", "row", "col", None),
        ),
        check_vma=False,
    )
```

```python
import jax
import jax.numpy as jnp
from jax import lax
from jax.experimental import pallas as pl
from jax.experimental.pallas import tpu as pltpu
from jax.sharding import PartitionSpec as P

def pair_kernel(pair_ref, dpair_ref, msg_ref, wp_ref, b_ref, mask_ref, aup_ref, adn_ref,
                *rest):
    out_ref, grad_ref, col_ref = rest[-3:]
    i = pl.program_id(1)
    ti, bc, dp = pair_ref.shape[1:]
    x = pair_ref[0]
    pre = jnp.dot(x.reshape(ti * bc, dp), wp_ref[...], preferred_element_type=jnp.float32)
    pre = pre.reshape(ti, bc, dp) + msg_ref[0][None] + b_ref[...][None]
    act = jnp.tanh(pre)
    out_ref[0] = (x.astype(jnp.float32) + act).astype(out_ref.dtype)
    d = dpair_ref[0].astype(jnp.float32)
    delta = (d * (1.0 - act * act)).astype(jnp.bfloat16)
    back = lax.dot_general(
        delta.reshape(ti * bc, dp), wp_ref[...], (((1,), (1,)), ((), ())),
        preferred_element_type=jnp.float32,
    )
    spread = jnp.where(mask_ref[...][None] > 0.5, aup_ref[0][:, None, :], adn_ref[0][:, None, :])
    grad_ref[0] = (d + back.reshape(ti, bc, dp) + spread).astype(grad_ref.dtype)
    part = jnp.sum(delta.astype(jnp.float32), axis=0)

    @pl.when(i == 0)
    def _():
        col_ref[0] = part

    @pl.when(i > 0)
    def _():
        col_ref[0] = col_ref[0] + part


def pair_pass(pair, d_pair, message_b, w_pair, b_pair, up_mask, a_up, a_down, first, prev=None):
    w, br, bc, dp = pair.shape
    group = message_b.shape[0]
    ti = max(1, min(br, 8192 // bc))
    grid = (group, br // ti)
    blk = pl.BlockSpec((1, ti, bc, dp), lambda a, i: (a + first, i, 0, 0))
    whole2 = lambda shape: pl.BlockSpec(shape, lambda a, i: (0, 0))
    per_w = pl.BlockSpec((1, bc, dp), lambda a, i: (a, 0, 0))
    rows = pl.BlockSpec((1, ti, dp), lambda a, i: (a, i, 0))
    in_specs = [blk, blk, per_w, whole2((dp, dp)), whole2((1, dp)),
                whole2((bc, dp)), rows, rows]
    args = [pair, d_pair, message_b, w_pair, b_pair.reshape(1, dp), up_mask, a_up, a_down]
    aliases = {}
    if prev is not None:
        in_specs += [pl.BlockSpec(memory_space=pl.ANY), pl.BlockSpec(memory_space=pl.ANY)]
        aliases = {len(args): 0, len(args) + 1: 1}
        args += list(prev)
    return pl.pallas_call(
        pair_kernel,
        grid=grid,
        in_specs=in_specs,
        out_specs=[blk, blk, per_w],
        out_shape=[jax.ShapeDtypeStruct(pair.shape, jnp.bfloat16),
                   jax.ShapeDtypeStruct(pair.shape, jnp.bfloat16),
                   jax.ShapeDtypeStruct((group, bc, dp), jnp.float32)],
        input_output_aliases=aliases,
        cost_estimate=pl.CostEstimate(
            flops=4 * group * br * bc * dp * dp,
            transcendentals=group * br * bc * dp,
            bytes_accessed=8 * group * br * bc * dp,
        ),
        compiler_params=pltpu.CompilerParams(dimension_semantics=("arbitrary", "arbitrary")),
    )(*args)


highest = lax.Precision.HIGHEST


def roll_pieces(pieces, shift):
    n = pieces.shape[0]
    doubled = jnp.concatenate([pieces, pieces], axis=0)
    return lax.dynamic_slice_in_dim(doubled, (n - shift) % n, n, 0)


def body(one_elec, pair, spins, w_single, b_single, w_pair, w_msg, b_pair, d_single, d_pair):
    walkers, block_rows, block_cols, width_pair = pair.shape
    own_rows = one_elec.shape[1]
    width_single = one_elec.shape[2]
    electrons = spins.shape[0]
    rows = electrons // block_rows
    cols = electrons // block_cols
    assert rows == cols
    pair_down = float(electrons) ** (-0.75)
    pair_boost = float(electrons) ** 0.75
    row_index = lax.axis_index("row")
    col_index = lax.axis_index("col")
    spin_up = spins.astype(jnp.float32)
    spin_down = 1.0 - spin_up
    count_up = jnp.sum(spin_up)
    count_down = float(electrons) - count_up
    spin_table = jnp.stack([spin_up, spin_down], axis=1)
    col_start = col_index * block_cols
    own_start = (row_index * cols + col_index) * own_rows
    col_table = lax.dynamic_slice_in_dim(spin_table, col_start, block_cols, 0)
    own_table = lax.dynamic_slice_in_dim(spin_table, own_start, own_rows, 0)

    both = ("row", "col")
    pieces = []
    for s in range(rows):
        perm = [(a * cols + b, ((b - s) % rows) * cols + a) for a in range(rows) for b in range(cols)]
        pieces.append(lax.ppermute(one_elec, both, perm))
    col_single = roll_pieces(jnp.stack(pieces), row_index)
    col_single = jnp.moveaxis(col_single, 0, 1).reshape(walkers, block_cols, width_single)

    col_spin_sums = jnp.einsum(
        "wjd,js->wsd", col_single, col_table.astype(jnp.bfloat16), preferred_element_type=jnp.float32
    )
    partial_value = jnp.einsum(
        "wijd,js->wisd", pair, col_table.astype(jnp.bfloat16), preferred_element_type=jnp.float32
    )
    sub_value = partial_value.reshape(walkers, cols, own_rows, 2, width_pair)
    own_sum = lax.dynamic_index_in_dim(sub_value, col_index, 1, keepdims=False)
    spin_sums = col_spin_sums
    spin_hi = col_spin_sums.astype(jnp.bfloat16)
    spin_lo = (col_spin_sums - spin_hi.astype(jnp.float32)).astype(jnp.bfloat16)
    split = own_rows * 2 * width_pair
    spin_size = 2 * width_single
    for s in range(1, cols):
        dest = col_index ^ s
        sent = lax.dynamic_index_in_dim(sub_value, dest, 1, keepdims=False)
        payload = jnp.concatenate(
            [
                sent.astype(jnp.bfloat16).reshape(walkers, -1),
                spin_hi.reshape(walkers, -1),
                spin_lo.reshape(walkers, -1),
            ],
            axis=1,
        )
        got = lax.ppermute(payload, "col", [(b, b ^ s) for b in range(cols)])
        own_sum = own_sum + got[:, :split].astype(jnp.float32).reshape(own_sum.shape)
        got_hi = got[:, split : split + spin_size].astype(jnp.float32)
        got_lo = got[:, split + spin_size :].astype(jnp.float32)
        spin_sums = spin_sums + (got_hi + got_lo).reshape(spin_sums.shape)

    single_wide = one_elec.astype(jnp.float32)
    features = jnp.concatenate(
        [
            single_wide,
            jnp.broadcast_to((spin_sums[:, 0, :] / count_up)[:, None], (walkers, own_rows, width_single)),
            jnp.broadcast_to((spin_sums[:, 1, :] / count_down)[:, None], (walkers, own_rows, width_single)),
            own_sum[:, :, 0, :] / count_up,
            own_sum[:, :, 1, :] / count_down,
        ],
        axis=2,
    ).astype(jnp.bfloat16)
    single_act = jnp.tanh(
        jnp.einsum("wif,fd->wid", features, w_single, preferred_element_type=jnp.float32) + b_single
    )
    single_out = (single_wide + single_act).astype(jnp.bfloat16)
    grad_pre = (d_single.astype(jnp.float32) * (1.0 - single_act * single_act)).astype(jnp.bfloat16)
    feature_grad = jnp.einsum("wid,fd->wif", grad_pre, w_single, preferred_element_type=jnp.float32)
    grad_direct = feature_grad[:, :, :width_single]
    grad_means = feature_grad[:, :, width_single : 3 * width_single].reshape(
        walkers, own_rows, 2, width_single
    )
    grad_pair_means = feature_grad[:, :, 3 * width_single :].reshape(
        walkers, own_rows, 2, width_pair
    )
    mean_sums = jnp.sum(grad_means, axis=1)

    mean_hi = mean_sums.astype(jnp.bfloat16)
    mean_lo = (mean_sums - mean_hi.astype(jnp.float32)).astype(jnp.bfloat16)
    payload = jnp.concatenate(
        [
            grad_pair_means.astype(jnp.bfloat16).reshape(walkers, -1),
            mean_hi.reshape(walkers, -1),
            mean_lo.reshape(walkers, -1),
        ],
        axis=1,
    )
    split = own_rows * 2 * width_pair
    mean_size = 2 * width_single
    gathered = [grad_pair_means.astype(jnp.bfloat16).astype(jnp.float32)] + [None] * (cols - 1)
    mean_part = mean_sums
    for s in range(1, cols):
        got = lax.ppermute(payload, "col", [(b, b ^ s) for b in range(cols)])
        gathered[s] = got[:, :split].astype(jnp.float32).reshape(grad_pair_means.shape)
        got_hi = got[:, split : split + mean_size].astype(jnp.float32)
        got_lo = got[:, split + mean_size :].astype(jnp.float32)
        mean_part = mean_part + (got_hi + got_lo).reshape(mean_sums.shape)
    gathered = jnp.stack(gathered)
    order = jnp.arange(cols) ^ col_index
    row_pair_grads = jnp.take(gathered, order, axis=0)
    row_pair_grads = jnp.moveaxis(row_pair_grads, 0, 1).reshape(walkers, block_rows, 2, width_pair)

    message = jnp.einsum("wjd,de->wje", col_single, w_msg, preferred_element_type=jnp.float32)
    a_up = pair_boost * (row_pair_grads[:, :, 0, :] / count_up)
    a_down = pair_boost * (row_pair_grads[:, :, 1, :] / count_down)
    up_mask = jnp.broadcast_to(col_table[:, :1], (block_cols, width_pair))
    pair_out, grad_pair, column_sum = pair_pass(
        pair, d_pair, message, w_pair, b_pair, up_mask, a_up, a_down, 0
    )

    sub_cols = column_sum.reshape(walkers, rows, own_rows, width_pair)
    mean_hi = mean_part.astype(jnp.bfloat16)
    mean_lo = (mean_part - mean_hi.astype(jnp.float32)).astype(jnp.bfloat16)
    split = own_rows * width_pair
    mean_size = 2 * width_single
    own_cols = None
    mean_total = None
    for s in range(rows):
        sent = lax.dynamic_index_in_dim(sub_cols, (row_index + s) % rows, 1, keepdims=False)
        payload = jnp.concatenate(
            [
                sent.astype(jnp.bfloat16).reshape(walkers, -1),
                mean_hi.reshape(walkers, -1),
                mean_lo.reshape(walkers, -1),
            ],
            axis=1,
        )
        perm = [(a * cols + b, b * cols + (a + s) % rows) for a in range(rows) for b in range(cols)]
        got = lax.ppermute(payload, both, perm)
        got_cols = got[:, :split].astype(jnp.float32).reshape(walkers, own_rows, width_pair)
        got_hi = got[:, split : split + mean_size].astype(jnp.float32)
        got_lo = got[:, split + mean_size :].astype(jnp.float32)
        got_mean = (got_hi + got_lo).reshape(mean_part.shape)
        own_cols = got_cols if own_cols is None else own_cols + got_cols
        mean_total = got_mean if mean_total is None else mean_total + got_mean

    own_message = pair_down * jnp.einsum(
        "wje,de->wjd", own_cols, w_msg.astype(jnp.float32), precision=highest
    )
    own_up = own_table[:, 0]
    own_down = own_table[:, 1]
    electron_grad = (
        own_up[None, :, None] * (mean_total[:, 0, :] / count_up)[:, None, :]
        + own_down[None, :, None] * (mean_total[:, 1, :] / count_down)[:, None, :]
        + own_message
    )
    grad_single = d_single.astype(jnp.float32) + grad_direct + electron_grad
    return (single_out, pair_out, grad_single, grad_pair)


def solution(mesh):
    placed = (
        P("walk", ("row", "col"), None),
        P("walk", "row", "col", None),
        P(),
        P(),
        P(),
        P(),
        P(),
        P(),
        P("walk", ("row", "col"), None),
        P("walk", "row", "col", None),
    )
    return jax.shard_map(
        body,
        mesh=mesh,
        in_specs=placed,
        out_specs=(
            P("walk", ("row", "col"), None),
            P("walk", "row", "col", None),
            P("walk", ("row", "col"), None),
            P("walk", "row", "col", None),
        ),
        check_vma=False,
    )
```

```python
import jax
import jax.numpy as jnp
from jax import lax
from jax.experimental import pallas as pl
from jax.experimental.pallas import tpu as pltpu
from jax.sharding import PartitionSpec as P

def pair_kernel(pair_ref, dpair_ref, msg_ref, wp_ref, b_ref, mask_ref, aup_ref, adn_ref,
                *rest):
    out_ref, grad_ref, col_ref = rest[-3:]
    i = pl.program_id(1)
    ti, bc, dp = pair_ref.shape[1:]
    x = pair_ref[0]
    pre = jnp.dot(x.reshape(ti * bc, dp), wp_ref[...], preferred_element_type=jnp.float32)
    pre = pre.reshape(ti, bc, dp) + msg_ref[0][None] + b_ref[...][None]
    act = jnp.tanh(pre)
    out_ref[0] = (x.astype(jnp.float32) + act).astype(out_ref.dtype)
    d = dpair_ref[0].astype(jnp.float32)
    delta = (d * (1.0 - act * act)).astype(jnp.bfloat16)
    back = lax.dot_general(
        delta.reshape(ti * bc, dp), wp_ref[...], (((1,), (1,)), ((), ())),
        preferred_element_type=jnp.float32,
    )
    spread = jnp.where(mask_ref[...][None] > 0.5, aup_ref[0][:, None, :], adn_ref[0][:, None, :])
    grad_ref[0] = (d + back.reshape(ti, bc, dp) + spread).astype(grad_ref.dtype)
    part = jnp.sum(delta.astype(jnp.float32), axis=0)

    @pl.when(i == 0)
    def _():
        col_ref[0] = part

    @pl.when(i > 0)
    def _():
        col_ref[0] = col_ref[0] + part


def pair_pass(pair, d_pair, message_b, w_pair, b_pair, up_mask, a_up, a_down, first, prev=None):
    w, br, bc, dp = pair.shape
    group = message_b.shape[0]
    ti = max(1, min(br, 8192 // bc))
    grid = (group, br // ti)
    blk = pl.BlockSpec((1, ti, bc, dp), lambda a, i: (a + first, i, 0, 0))
    whole2 = lambda shape: pl.BlockSpec(shape, lambda a, i: (0, 0))
    per_w = pl.BlockSpec((1, bc, dp), lambda a, i: (a, 0, 0))
    rows = pl.BlockSpec((1, ti, dp), lambda a, i: (a, i, 0))
    in_specs = [blk, blk, per_w, whole2((dp, dp)), whole2((1, dp)),
                whole2((bc, 1)), rows, rows]
    args = [pair, d_pair, message_b, w_pair, b_pair.reshape(1, dp), up_mask, a_up, a_down]
    aliases = {}
    if prev is not None:
        in_specs += [pl.BlockSpec(memory_space=pl.ANY), pl.BlockSpec(memory_space=pl.ANY)]
        aliases = {len(args): 0, len(args) + 1: 1}
        args += list(prev)
    return pl.pallas_call(
        pair_kernel,
        grid=grid,
        in_specs=in_specs,
        out_specs=[blk, blk, per_w],
        out_shape=[jax.ShapeDtypeStruct(pair.shape, jnp.bfloat16),
                   jax.ShapeDtypeStruct(pair.shape, jnp.bfloat16),
                   jax.ShapeDtypeStruct((group, bc, dp), jnp.float32)],
        input_output_aliases=aliases,
        cost_estimate=pl.CostEstimate(
            flops=4 * group * br * bc * dp * dp,
            transcendentals=group * br * bc * dp,
            bytes_accessed=8 * group * br * bc * dp,
        ),
        compiler_params=pltpu.CompilerParams(dimension_semantics=("arbitrary", "arbitrary")),
    )(*args)


highest = lax.Precision.HIGHEST


def roll_pieces(pieces, shift):
    n = pieces.shape[0]
    doubled = jnp.concatenate([pieces, pieces], axis=0)
    return lax.dynamic_slice_in_dim(doubled, (n - shift) % n, n, 0)


def body(one_elec, pair, spins, w_single, b_single, w_pair, w_msg, b_pair, d_single, d_pair):
    walkers, block_rows, block_cols, width_pair = pair.shape
    own_rows = one_elec.shape[1]
    width_single = one_elec.shape[2]
    electrons = spins.shape[0]
    rows = electrons // block_rows
    cols = electrons // block_cols
    assert rows == cols
    pair_down = float(electrons) ** (-0.75)
    pair_boost = float(electrons) ** 0.75
    row_index = lax.axis_index("row")
    col_index = lax.axis_index("col")
    spin_up = spins.astype(jnp.float32)
    spin_down = 1.0 - spin_up
    count_up = jnp.sum(spin_up)
    count_down = float(electrons) - count_up
    spin_table = jnp.stack([spin_up, spin_down], axis=1)
    col_start = col_index * block_cols
    own_start = (row_index * cols + col_index) * own_rows
    col_table = lax.dynamic_slice_in_dim(spin_table, col_start, block_cols, 0)
    own_table = lax.dynamic_slice_in_dim(spin_table, own_start, own_rows, 0)

    both = ("row", "col")
    pieces = []
    for s in range(rows):
        perm = [(a * cols + b, ((b - s) % rows) * cols + a) for a in range(rows) for b in range(cols)]
        pieces.append(lax.ppermute(one_elec, both, perm))
    col_single = roll_pieces(jnp.stack(pieces), row_index)
    col_single = jnp.moveaxis(col_single, 0, 1).reshape(walkers, block_cols, width_single)

    col_spin_sums = jnp.einsum(
        "wjd,js->wsd", col_single, col_table.astype(jnp.bfloat16), preferred_element_type=jnp.float32
    )
    partial_value = jnp.einsum(
        "wijd,js->wisd", pair, col_table.astype(jnp.bfloat16), preferred_element_type=jnp.float32
    )
    sub_value = partial_value.reshape(walkers, cols, own_rows, 2, width_pair)
    own_sum = lax.dynamic_index_in_dim(sub_value, col_index, 1, keepdims=False)
    spin_sums = col_spin_sums
    spin_hi = col_spin_sums.astype(jnp.bfloat16)
    spin_lo = (col_spin_sums - spin_hi.astype(jnp.float32)).astype(jnp.bfloat16)
    split = own_rows * 2 * width_pair
    spin_size = 2 * width_single
    for s in range(1, cols):
        dest = col_index ^ s
        sent = lax.dynamic_index_in_dim(sub_value, dest, 1, keepdims=False)
        payload = jnp.concatenate(
            [
                sent.astype(jnp.bfloat16).reshape(walkers, -1),
                spin_hi.reshape(walkers, -1),
                spin_lo.reshape(walkers, -1),
            ],
            axis=1,
        )
        got = lax.ppermute(payload, "col", [(b, b ^ s) for b in range(cols)])
        own_sum = own_sum + got[:, :split].astype(jnp.float32).reshape(own_sum.shape)
        got_hi = got[:, split : split + spin_size].astype(jnp.float32)
        got_lo = got[:, split + spin_size :].astype(jnp.float32)
        spin_sums = spin_sums + (got_hi + got_lo).reshape(spin_sums.shape)

    single_wide = one_elec.astype(jnp.float32)
    features = jnp.concatenate(
        [
            single_wide,
            jnp.broadcast_to((spin_sums[:, 0, :] / count_up)[:, None], (walkers, own_rows, width_single)),
            jnp.broadcast_to((spin_sums[:, 1, :] / count_down)[:, None], (walkers, own_rows, width_single)),
            own_sum[:, :, 0, :] / count_up,
            own_sum[:, :, 1, :] / count_down,
        ],
        axis=2,
    ).astype(jnp.bfloat16)
    single_act = jnp.tanh(
        jnp.einsum("wif,fd->wid", features, w_single, preferred_element_type=jnp.float32) + b_single
    )
    single_out = (single_wide + single_act).astype(jnp.bfloat16)
    grad_pre = (d_single.astype(jnp.float32) * (1.0 - single_act * single_act)).astype(jnp.bfloat16)
    feature_grad = jnp.einsum("wid,fd->wif", grad_pre, w_single, preferred_element_type=jnp.float32)
    grad_direct = feature_grad[:, :, :width_single]
    grad_means = feature_grad[:, :, width_single : 3 * width_single].reshape(
        walkers, own_rows, 2, width_single
    )
    grad_pair_means = feature_grad[:, :, 3 * width_single :].reshape(
        walkers, own_rows, 2, width_pair
    )
    mean_sums = jnp.sum(grad_means, axis=1)

    mean_hi = mean_sums.astype(jnp.bfloat16)
    mean_lo = (mean_sums - mean_hi.astype(jnp.float32)).astype(jnp.bfloat16)
    payload = jnp.concatenate(
        [
            grad_pair_means.astype(jnp.bfloat16).reshape(walkers, -1),
            mean_hi.reshape(walkers, -1),
            mean_lo.reshape(walkers, -1),
        ],
        axis=1,
    )
    split = own_rows * 2 * width_pair
    mean_size = 2 * width_single
    gathered = [grad_pair_means.astype(jnp.bfloat16).astype(jnp.float32)] + [None] * (cols - 1)
    mean_part = mean_sums
    for s in range(1, cols):
        got = lax.ppermute(payload, "col", [(b, b ^ s) for b in range(cols)])
        gathered[s] = got[:, :split].astype(jnp.float32).reshape(grad_pair_means.shape)
        got_hi = got[:, split : split + mean_size].astype(jnp.float32)
        got_lo = got[:, split + mean_size :].astype(jnp.float32)
        mean_part = mean_part + (got_hi + got_lo).reshape(mean_sums.shape)
    ordered = []
    for m in range(cols):
        pick = gathered[0]
        for s in range(1, cols):
            pick = jnp.where((col_index ^ m) == s, gathered[s], pick)
        ordered.append(pick)
    row_pair_grads = jnp.stack(ordered, axis=1).reshape(walkers, block_rows, 2, width_pair)

    message = jnp.einsum("wjd,de->wje", col_single, w_msg, preferred_element_type=jnp.float32)
    a_up = pair_boost * (row_pair_grads[:, :, 0, :] / count_up)
    a_down = pair_boost * (row_pair_grads[:, :, 1, :] / count_down)
    up_mask = col_table[:, :1]
    pair_out, grad_pair, column_sum = pair_pass(
        pair, d_pair, message, w_pair, b_pair, up_mask, a_up, a_down, 0
    )

    sub_cols = column_sum.reshape(walkers, rows, own_rows, width_pair)
    mean_hi = mean_part.astype(jnp.bfloat16)
    mean_lo = (mean_part - mean_hi.astype(jnp.float32)).astype(jnp.bfloat16)
    split = own_rows * width_pair
    mean_size = 2 * width_single
    own_cols = None
    mean_total = None
    for s in range(rows):
        sent = lax.dynamic_index_in_dim(sub_cols, (row_index + s) % rows, 1, keepdims=False)
        payload = jnp.concatenate(
            [
                sent.astype(jnp.bfloat16).reshape(walkers, -1),
                mean_hi.reshape(walkers, -1),
                mean_lo.reshape(walkers, -1),
            ],
            axis=1,
        )
        perm = [(a * cols + b, b * cols + (a + s) % rows) for a in range(rows) for b in range(cols)]
        got = lax.ppermute(payload, both, perm)
        got_cols = got[:, :split].astype(jnp.float32).reshape(walkers, own_rows, width_pair)
        got_hi = got[:, split : split + mean_size].astype(jnp.float32)
        got_lo = got[:, split + mean_size :].astype(jnp.float32)
        got_mean = (got_hi + got_lo).reshape(mean_part.shape)
        own_cols = got_cols if own_cols is None else own_cols + got_cols
        mean_total = got_mean if mean_total is None else mean_total + got_mean

    own_message = pair_down * jnp.einsum(
        "wje,de->wjd", own_cols, w_msg.astype(jnp.float32), precision=highest
    )
    own_up = own_table[:, 0]
    own_down = own_table[:, 1]
    electron_grad = (
        own_up[None, :, None] * (mean_total[:, 0, :] / count_up)[:, None, :]
        + own_down[None, :, None] * (mean_total[:, 1, :] / count_down)[:, None, :]
        + own_message
    )
    grad_single = d_single.astype(jnp.float32) + grad_direct + electron_grad
    return (single_out, pair_out, grad_single, grad_pair)


def solution(mesh):
    placed = (
        P("walk", ("row", "col"), None),
        P("walk", "row", "col", None),
        P(),
        P(),
        P(),
        P(),
        P(),
        P(),
        P("walk", ("row", "col"), None),
        P("walk", "row", "col", None),
    )
    return jax.shard_map(
        body,
        mesh=mesh,
        in_specs=placed,
        out_specs=(
            P("walk", ("row", "col"), None),
            P("walk", "row", "col", None),
            P("walk", ("row", "col"), None),
            P("walk", "row", "col", None),
        ),
        check_vma=False,
    )
```

```python
import jax
import jax.numpy as jnp
from jax import lax
from jax.experimental import pallas as pl
from jax.experimental.pallas import tpu as pltpu
from jax.sharding import PartitionSpec as P

def pair_kernel(pair_ref, dpair_ref, msg_ref, wp_ref, b_ref, mask_ref, aup_ref, adn_ref,
                *rest):
    out_ref, grad_ref, col_ref = rest[-3:]
    i = pl.program_id(1)
    ti, bc, dp = pair_ref.shape[1:]
    x = pair_ref[0]
    pre = jnp.dot(x.reshape(ti * bc, dp), wp_ref[...], preferred_element_type=jnp.float32)
    pre = pre.reshape(ti, bc, dp) + msg_ref[0][None] + b_ref[...][None]
    act = jnp.tanh(pre)
    out_ref[0] = (x.astype(jnp.float32) + act).astype(out_ref.dtype)
    d = dpair_ref[0].astype(jnp.float32)
    delta = (d * (1.0 - act * act)).astype(jnp.bfloat16)
    back = lax.dot_general(
        delta.reshape(ti * bc, dp), wp_ref[...], (((1,), (1,)), ((), ())),
        preferred_element_type=jnp.float32,
    )
    spread = jnp.where(mask_ref[...][None] > 0.5, aup_ref[0][:, None, :], adn_ref[0][:, None, :])
    grad_ref[0] = (d + back.reshape(ti, bc, dp) + spread).astype(grad_ref.dtype)
    part = jnp.sum(delta.astype(jnp.float32), axis=0)

    @pl.when(i == 0)
    def _():
        col_ref[0] = part

    @pl.when(i > 0)
    def _():
        col_ref[0] = col_ref[0] + part


def pair_pass(pair, d_pair, message_b, w_pair, b_pair, up_mask, a_up, a_down, first, prev=None):
    w, br, bc, dp = pair.shape
    group = message_b.shape[0]
    ti = max(1, min(br, 8192 // bc))
    grid = (group, br // ti)
    blk = pl.BlockSpec((1, ti, bc, dp), lambda a, i: (a + first, i, 0, 0))
    whole2 = lambda shape: pl.BlockSpec(shape, lambda a, i: (0, 0))
    per_w = pl.BlockSpec((1, bc, dp), lambda a, i: (a, 0, 0))
    rows = pl.BlockSpec((1, ti, dp), lambda a, i: (a, i, 0))
    in_specs = [blk, blk, per_w, whole2((dp, dp)), whole2((1, dp)),
                whole2((bc, 1)), rows, rows]
    args = [pair, d_pair, message_b, w_pair, b_pair.reshape(1, dp), up_mask, a_up, a_down]
    aliases = {}
    if prev is not None:
        in_specs += [pl.BlockSpec(memory_space=pl.ANY), pl.BlockSpec(memory_space=pl.ANY)]
        aliases = {len(args): 0, len(args) + 1: 1}
        args += list(prev)
    return pl.pallas_call(
        pair_kernel,
        grid=grid,
        in_specs=in_specs,
        out_specs=[blk, blk, per_w],
        out_shape=[jax.ShapeDtypeStruct(pair.shape, jnp.bfloat16),
                   jax.ShapeDtypeStruct(pair.shape, jnp.bfloat16),
                   jax.ShapeDtypeStruct((group, bc, dp), jnp.float32)],
        input_output_aliases=aliases,
        cost_estimate=pl.CostEstimate(
            flops=4 * group * br * bc * dp * dp,
            transcendentals=group * br * bc * dp,
            bytes_accessed=8 * group * br * bc * dp,
        ),
        compiler_params=pltpu.CompilerParams(dimension_semantics=("arbitrary", "arbitrary")),
    )(*args)


highest = lax.Precision.HIGHEST


def roll_pieces(pieces, shift):
    n = pieces.shape[0]
    doubled = jnp.concatenate([pieces, pieces], axis=0)
    return lax.dynamic_slice_in_dim(doubled, (n - shift) % n, n, 0)


def body(one_elec, pair, spins, w_single, b_single, w_pair, w_msg, b_pair, d_single, d_pair):
    walkers, block_rows, block_cols, width_pair = pair.shape
    own_rows = one_elec.shape[1]
    width_single = one_elec.shape[2]
    electrons = spins.shape[0]
    rows = electrons // block_rows
    cols = electrons // block_cols
    assert rows == cols
    pair_down = float(electrons) ** (-0.75)
    pair_boost = float(electrons) ** 0.75
    row_index = lax.axis_index("row")
    col_index = lax.axis_index("col")
    spin_up = spins.astype(jnp.float32)
    spin_down = 1.0 - spin_up
    count_up = jnp.sum(spin_up)
    count_down = float(electrons) - count_up
    spin_table = jnp.stack([spin_up, spin_down], axis=1)
    col_start = col_index * block_cols
    own_start = (row_index * cols + col_index) * own_rows
    col_table = lax.dynamic_slice_in_dim(spin_table, col_start, block_cols, 0)
    own_table = lax.dynamic_slice_in_dim(spin_table, own_start, own_rows, 0)

    both = ("row", "col")
    pieces = []
    for s in range(rows):
        perm = [(a * cols + b, ((b - s) % rows) * cols + a) for a in range(rows) for b in range(cols)]
        pieces.append(lax.ppermute(one_elec, both, perm))
    col_single = roll_pieces(jnp.stack(pieces), row_index)
    col_single = jnp.moveaxis(col_single, 0, 1).reshape(walkers, block_cols, width_single)

    col_spin_sums = jnp.einsum(
        "wjd,js->wsd", col_single, col_table.astype(jnp.bfloat16), preferred_element_type=jnp.float32
    )
    col_bf = col_table.astype(jnp.bfloat16)

    def pair_spin_sums(block):
        chunk = lax.dynamic_slice_in_dim(pair, block * own_rows, own_rows, 1)
        return jnp.einsum("wijd,js->wisd", chunk, col_bf, preferred_element_type=jnp.float32)

    spin_sums = col_spin_sums
    own_sum = None
    spin_hi = col_spin_sums.astype(jnp.bfloat16)
    spin_lo = (col_spin_sums - spin_hi.astype(jnp.float32)).astype(jnp.bfloat16)
    split = own_rows * 2 * width_pair
    spin_size = 2 * width_single
    for s in range(1, cols):
        dest = col_index ^ s
        sent = pair_spin_sums(dest)
        payload = jnp.concatenate(
            [
                sent.astype(jnp.bfloat16).reshape(walkers, -1),
                spin_hi.reshape(walkers, -1),
                spin_lo.reshape(walkers, -1),
            ],
            axis=1,
        )
        got = lax.ppermute(payload, "col", [(b, b ^ s) for b in range(cols)])
        got_sum = got[:, :split].astype(jnp.float32).reshape(walkers, own_rows, 2, width_pair)
        own_sum = got_sum if own_sum is None else own_sum + got_sum
        got_hi = got[:, split : split + spin_size].astype(jnp.float32)
        got_lo = got[:, split + spin_size :].astype(jnp.float32)
        spin_sums = spin_sums + (got_hi + got_lo).reshape(spin_sums.shape)
    own_sum = own_sum + pair_spin_sums(col_index)

    single_wide = one_elec.astype(jnp.float32)
    features = jnp.concatenate(
        [
            single_wide,
            jnp.broadcast_to((spin_sums[:, 0, :] / count_up)[:, None], (walkers, own_rows, width_single)),
            jnp.broadcast_to((spin_sums[:, 1, :] / count_down)[:, None], (walkers, own_rows, width_single)),
            own_sum[:, :, 0, :] / count_up,
            own_sum[:, :, 1, :] / count_down,
        ],
        axis=2,
    ).astype(jnp.bfloat16)
    single_act = jnp.tanh(
        jnp.einsum("wif,fd->wid", features, w_single, preferred_element_type=jnp.float32) + b_single
    )
    single_out = (single_wide + single_act).astype(jnp.bfloat16)
    grad_pre = (d_single.astype(jnp.float32) * (1.0 - single_act * single_act)).astype(jnp.bfloat16)
    feature_grad = jnp.einsum("wid,fd->wif", grad_pre, w_single, preferred_element_type=jnp.float32)
    grad_direct = feature_grad[:, :, :width_single]
    grad_means = feature_grad[:, :, width_single : 3 * width_single].reshape(
        walkers, own_rows, 2, width_single
    )
    grad_pair_means = feature_grad[:, :, 3 * width_single :].reshape(
        walkers, own_rows, 2, width_pair
    )
    mean_sums = jnp.sum(grad_means, axis=1)

    mean_hi = mean_sums.astype(jnp.bfloat16)
    mean_lo = (mean_sums - mean_hi.astype(jnp.float32)).astype(jnp.bfloat16)
    payload = jnp.concatenate(
        [
            grad_pair_means.astype(jnp.bfloat16).reshape(walkers, -1),
            mean_hi.reshape(walkers, -1),
            mean_lo.reshape(walkers, -1),
        ],
        axis=1,
    )
    split = own_rows * 2 * width_pair
    mean_size = 2 * width_single
    gathered = [grad_pair_means.astype(jnp.bfloat16).astype(jnp.float32)] + [None] * (cols - 1)
    mean_part = mean_sums
    for s in range(1, cols):
        got = lax.ppermute(payload, "col", [(b, b ^ s) for b in range(cols)])
        gathered[s] = got[:, :split].astype(jnp.float32).reshape(grad_pair_means.shape)
        got_hi = got[:, split : split + mean_size].astype(jnp.float32)
        got_lo = got[:, split + mean_size :].astype(jnp.float32)
        mean_part = mean_part + (got_hi + got_lo).reshape(mean_sums.shape)
    ordered = []
    for m in range(cols):
        pick = gathered[0]
        for s in range(1, cols):
            pick = jnp.where((col_index ^ m) == s, gathered[s], pick)
        ordered.append(pick)
    row_pair_grads = jnp.stack(ordered, axis=1).reshape(walkers, block_rows, 2, width_pair)

    message = jnp.einsum("wjd,de->wje", col_single, w_msg, preferred_element_type=jnp.float32)
    a_up = pair_boost * (row_pair_grads[:, :, 0, :] / count_up)
    a_down = pair_boost * (row_pair_grads[:, :, 1, :] / count_down)
    up_mask = col_table[:, :1]
    pair_out, grad_pair, column_sum = pair_pass(
        pair, d_pair, message, w_pair, b_pair, up_mask, a_up, a_down, 0
    )

    sub_cols = column_sum.reshape(walkers, rows, own_rows, width_pair)
    mean_hi = mean_part.astype(jnp.bfloat16)
    mean_lo = (mean_part - mean_hi.astype(jnp.float32)).astype(jnp.bfloat16)
    split = own_rows * width_pair
    mean_size = 2 * width_single
    own_cols = None
    mean_total = None
    for s in range(rows):
        sent = lax.dynamic_index_in_dim(sub_cols, (row_index + s) % rows, 1, keepdims=False)
        payload = jnp.concatenate(
            [
                sent.astype(jnp.bfloat16).reshape(walkers, -1),
                mean_hi.reshape(walkers, -1),
                mean_lo.reshape(walkers, -1),
            ],
            axis=1,
        )
        perm = [(a * cols + b, b * cols + (a + s) % rows) for a in range(rows) for b in range(cols)]
        got = lax.ppermute(payload, both, perm)
        got_cols = got[:, :split].astype(jnp.float32).reshape(walkers, own_rows, width_pair)
        got_hi = got[:, split : split + mean_size].astype(jnp.float32)
        got_lo = got[:, split + mean_size :].astype(jnp.float32)
        got_mean = (got_hi + got_lo).reshape(mean_part.shape)
        own_cols = got_cols if own_cols is None else own_cols + got_cols
        mean_total = got_mean if mean_total is None else mean_total + got_mean

    own_message = pair_down * jnp.einsum(
        "wje,de->wjd", own_cols, w_msg.astype(jnp.float32), precision=highest
    )
    own_up = own_table[:, 0]
    own_down = own_table[:, 1]
    electron_grad = (
        own_up[None, :, None] * (mean_total[:, 0, :] / count_up)[:, None, :]
        + own_down[None, :, None] * (mean_total[:, 1, :] / count_down)[:, None, :]
        + own_message
    )
    grad_single = d_single.astype(jnp.float32) + grad_direct + electron_grad
    return (single_out, pair_out, grad_single, grad_pair)


def solution(mesh):
    placed = (
        P("walk", ("row", "col"), None),
        P("walk", "row", "col", None),
        P(),
        P(),
        P(),
        P(),
        P(),
        P(),
        P("walk", ("row", "col"), None),
        P("walk", "row", "col", None),
    )
    return jax.shard_map(
        body,
        mesh=mesh,
        in_specs=placed,
        out_specs=(
            P("walk", ("row", "col"), None),
            P("walk", "row", "col", None),
            P("walk", ("row", "col"), None),
            P("walk", "row", "col", None),
        ),
        check_vma=False,
    )
```

```python
import jax
import jax.numpy as jnp
from jax import lax
from jax.experimental import pallas as pl
from jax.experimental.pallas import tpu as pltpu
from jax.sharding import PartitionSpec as P

def pair_kernel(pair_ref, dpair_ref, single_ref, wmsg_ref, wp_ref, b_ref, mask_ref, aup_ref,
                adn_ref, *rest):
    out_ref, grad_ref, col_ref, msg_scr = rest[-4:]
    i = pl.program_id(1)
    ti, bc, dp = pair_ref.shape[1:]

    @pl.when(i == 0)
    def _():
        msg_scr[...] = jnp.dot(single_ref[0], wmsg_ref[...], preferred_element_type=jnp.float32)

    x = pair_ref[0]
    pre = jnp.dot(x.reshape(ti * bc, dp), wp_ref[...], preferred_element_type=jnp.float32)
    pre = pre.reshape(ti, bc, dp) + msg_scr[...][None] + b_ref[...][None]
    act = jnp.tanh(pre)
    out_ref[0] = (x.astype(jnp.float32) + act).astype(out_ref.dtype)
    d = dpair_ref[0].astype(jnp.float32)
    delta = (d * (1.0 - act * act)).astype(jnp.bfloat16)
    back = lax.dot_general(
        delta.reshape(ti * bc, dp), wp_ref[...], (((1,), (1,)), ((), ())),
        preferred_element_type=jnp.float32,
    )
    spread = jnp.where(mask_ref[...][None] > 0.5, aup_ref[0][:, None, :], adn_ref[0][:, None, :])
    grad_ref[0] = (d + back.reshape(ti, bc, dp) + spread).astype(grad_ref.dtype)
    part = jnp.sum(delta.astype(jnp.float32), axis=0)

    @pl.when(i == 0)
    def _():
        col_ref[0] = part

    @pl.when(i > 0)
    def _():
        col_ref[0] = col_ref[0] + part


def pair_pass(pair, d_pair, col_single, w_msg, w_pair, b_pair, up_mask, a_up, a_down, first,
              prev=None):
    w, br, bc, dp = pair.shape
    group = col_single.shape[0]
    ds = col_single.shape[2]
    ti = max(1, min(br, 8192 // bc))
    grid = (group, br // ti)
    blk = pl.BlockSpec((1, ti, bc, dp), lambda a, i: (a + first, i, 0, 0))
    whole2 = lambda shape: pl.BlockSpec(shape, lambda a, i: (0, 0))
    per_w = pl.BlockSpec((1, bc, dp), lambda a, i: (a, 0, 0))
    rows = pl.BlockSpec((1, ti, dp), lambda a, i: (a, i, 0))
    per_w_single = pl.BlockSpec((1, bc, ds), lambda a, i: (a, 0, 0))
    in_specs = [blk, blk, per_w_single, whole2((ds, dp)), whole2((dp, dp)), whole2((1, dp)),
                whole2((bc, 1)), rows, rows]
    args = [pair, d_pair, col_single, w_msg, w_pair, b_pair.reshape(1, dp), up_mask, a_up, a_down]
    aliases = {}
    if prev is not None:
        in_specs += [pl.BlockSpec(memory_space=pl.ANY), pl.BlockSpec(memory_space=pl.ANY)]
        aliases = {len(args): 0, len(args) + 1: 1}
        args += list(prev)
    return pl.pallas_call(
        pair_kernel,
        grid=grid,
        in_specs=in_specs,
        out_specs=[blk, blk, per_w],
        out_shape=[jax.ShapeDtypeStruct(pair.shape, jnp.bfloat16),
                   jax.ShapeDtypeStruct(pair.shape, jnp.bfloat16),
                   jax.ShapeDtypeStruct((group, bc, dp), jnp.float32)],
        scratch_shapes=[pltpu.VMEM((bc, dp), jnp.float32)],
        input_output_aliases=aliases,
        cost_estimate=pl.CostEstimate(
            flops=4 * group * br * bc * dp * dp,
            transcendentals=group * br * bc * dp,
            bytes_accessed=8 * group * br * bc * dp,
        ),
        compiler_params=pltpu.CompilerParams(dimension_semantics=("arbitrary", "arbitrary")),
    )(*args)


highest = lax.Precision.HIGHEST


def roll_pieces(pieces, shift):
    n = pieces.shape[0]
    doubled = jnp.concatenate([pieces, pieces], axis=0)
    return lax.dynamic_slice_in_dim(doubled, (n - shift) % n, n, 0)


def body(one_elec, pair, spins, w_single, b_single, w_pair, w_msg, b_pair, d_single, d_pair):
    walkers, block_rows, block_cols, width_pair = pair.shape
    own_rows = one_elec.shape[1]
    width_single = one_elec.shape[2]
    electrons = spins.shape[0]
    rows = electrons // block_rows
    cols = electrons // block_cols
    assert rows == cols
    pair_down = float(electrons) ** (-0.75)
    pair_boost = float(electrons) ** 0.75
    row_index = lax.axis_index("row")
    col_index = lax.axis_index("col")
    spin_up = spins.astype(jnp.float32)
    spin_down = 1.0 - spin_up
    count_up = jnp.sum(spin_up)
    count_down = float(electrons) - count_up
    spin_table = jnp.stack([spin_up, spin_down], axis=1)
    col_start = col_index * block_cols
    own_start = (row_index * cols + col_index) * own_rows
    col_table = lax.dynamic_slice_in_dim(spin_table, col_start, block_cols, 0)
    own_table = lax.dynamic_slice_in_dim(spin_table, own_start, own_rows, 0)

    both = ("row", "col")
    pieces = []
    for s in range(rows):
        perm = [(a * cols + b, ((b - s) % rows) * cols + a) for a in range(rows) for b in range(cols)]
        pieces.append(lax.ppermute(one_elec, both, perm))
    col_single = roll_pieces(jnp.stack(pieces), row_index)
    col_single = jnp.moveaxis(col_single, 0, 1).reshape(walkers, block_cols, width_single)

    col_spin_sums = jnp.einsum(
        "wjd,js->wsd", col_single, col_table.astype(jnp.bfloat16), preferred_element_type=jnp.float32
    )
    partial_value = jnp.einsum(
        "wijd,js->wisd", pair, col_table.astype(jnp.bfloat16), preferred_element_type=jnp.float32
    )
    sub_value = partial_value.reshape(walkers, cols, own_rows, 2, width_pair)
    own_sum = lax.dynamic_index_in_dim(sub_value, col_index, 1, keepdims=False)
    spin_sums = col_spin_sums
    spin_hi = col_spin_sums.astype(jnp.bfloat16)
    spin_lo = (col_spin_sums - spin_hi.astype(jnp.float32)).astype(jnp.bfloat16)
    split = own_rows * 2 * width_pair
    spin_size = 2 * width_single
    for s in range(1, cols):
        dest = col_index ^ s
        sent = lax.dynamic_index_in_dim(sub_value, dest, 1, keepdims=False)
        payload = jnp.concatenate(
            [
                sent.astype(jnp.bfloat16).reshape(walkers, -1),
                spin_hi.reshape(walkers, -1),
                spin_lo.reshape(walkers, -1),
            ],
            axis=1,
        )
        got = lax.ppermute(payload, "col", [(b, b ^ s) for b in range(cols)])
        own_sum = own_sum + got[:, :split].astype(jnp.float32).reshape(own_sum.shape)
        got_hi = got[:, split : split + spin_size].astype(jnp.float32)
        got_lo = got[:, split + spin_size :].astype(jnp.float32)
        spin_sums = spin_sums + (got_hi + got_lo).reshape(spin_sums.shape)

    single_wide = one_elec.astype(jnp.float32)
    features = jnp.concatenate(
        [
            single_wide,
            jnp.broadcast_to((spin_sums[:, 0, :] / count_up)[:, None], (walkers, own_rows, width_single)),
            jnp.broadcast_to((spin_sums[:, 1, :] / count_down)[:, None], (walkers, own_rows, width_single)),
            own_sum[:, :, 0, :] / count_up,
            own_sum[:, :, 1, :] / count_down,
        ],
        axis=2,
    ).astype(jnp.bfloat16)
    single_act = jnp.tanh(
        jnp.einsum("wif,fd->wid", features, w_single, preferred_element_type=jnp.float32) + b_single
    )
    single_out = (single_wide + single_act).astype(jnp.bfloat16)
    grad_pre = (d_single.astype(jnp.float32) * (1.0 - single_act * single_act)).astype(jnp.bfloat16)
    feature_grad = jnp.einsum("wid,fd->wif", grad_pre, w_single, preferred_element_type=jnp.float32)
    grad_direct = feature_grad[:, :, :width_single]
    grad_means = feature_grad[:, :, width_single : 3 * width_single].reshape(
        walkers, own_rows, 2, width_single
    )
    grad_pair_means = feature_grad[:, :, 3 * width_single :].reshape(
        walkers, own_rows, 2, width_pair
    )
    mean_sums = jnp.sum(grad_means, axis=1)

    mean_hi = mean_sums.astype(jnp.bfloat16)
    mean_lo = (mean_sums - mean_hi.astype(jnp.float32)).astype(jnp.bfloat16)
    payload = jnp.concatenate(
        [
            grad_pair_means.astype(jnp.bfloat16).reshape(walkers, -1),
            mean_hi.reshape(walkers, -1),
            mean_lo.reshape(walkers, -1),
        ],
        axis=1,
    )
    split = own_rows * 2 * width_pair
    mean_size = 2 * width_single
    gathered = [grad_pair_means.astype(jnp.bfloat16).astype(jnp.float32)] + [None] * (cols - 1)
    mean_part = mean_sums
    for s in range(1, cols):
        got = lax.ppermute(payload, "col", [(b, b ^ s) for b in range(cols)])
        gathered[s] = got[:, :split].astype(jnp.float32).reshape(grad_pair_means.shape)
        got_hi = got[:, split : split + mean_size].astype(jnp.float32)
        got_lo = got[:, split + mean_size :].astype(jnp.float32)
        mean_part = mean_part + (got_hi + got_lo).reshape(mean_sums.shape)
    ordered = []
    for m in range(cols):
        pick = gathered[0]
        for s in range(1, cols):
            pick = jnp.where((col_index ^ m) == s, gathered[s], pick)
        ordered.append(pick)
    row_pair_grads = jnp.stack(ordered, axis=1).reshape(walkers, block_rows, 2, width_pair)

    a_up = pair_boost * (row_pair_grads[:, :, 0, :] / count_up)
    a_down = pair_boost * (row_pair_grads[:, :, 1, :] / count_down)
    up_mask = col_table[:, :1]
    pair_out, grad_pair, column_sum = pair_pass(
        pair, d_pair, col_single, w_msg, w_pair, b_pair, up_mask, a_up, a_down, 0
    )

    sub_cols = column_sum.reshape(walkers, rows, own_rows, width_pair)
    mean_hi = mean_part.astype(jnp.bfloat16)
    mean_lo = (mean_part - mean_hi.astype(jnp.float32)).astype(jnp.bfloat16)
    split = own_rows * width_pair
    mean_size = 2 * width_single
    own_cols = None
    mean_total = None
    for s in range(rows):
        sent = lax.dynamic_index_in_dim(sub_cols, (row_index + s) % rows, 1, keepdims=False)
        payload = jnp.concatenate(
            [
                sent.astype(jnp.bfloat16).reshape(walkers, -1),
                mean_hi.reshape(walkers, -1),
                mean_lo.reshape(walkers, -1),
            ],
            axis=1,
        )
        perm = [(a * cols + b, b * cols + (a + s) % rows) for a in range(rows) for b in range(cols)]
        got = lax.ppermute(payload, both, perm)
        got_cols = got[:, :split].astype(jnp.float32).reshape(walkers, own_rows, width_pair)
        got_hi = got[:, split : split + mean_size].astype(jnp.float32)
        got_lo = got[:, split + mean_size :].astype(jnp.float32)
        got_mean = (got_hi + got_lo).reshape(mean_part.shape)
        own_cols = got_cols if own_cols is None else own_cols + got_cols
        mean_total = got_mean if mean_total is None else mean_total + got_mean

    own_message = pair_down * jnp.einsum(
        "wje,de->wjd", own_cols, w_msg.astype(jnp.float32), precision=highest
    )
    own_up = own_table[:, 0]
    own_down = own_table[:, 1]
    electron_grad = (
        own_up[None, :, None] * (mean_total[:, 0, :] / count_up)[:, None, :]
        + own_down[None, :, None] * (mean_total[:, 1, :] / count_down)[:, None, :]
        + own_message
    )
    grad_single = d_single.astype(jnp.float32) + grad_direct + electron_grad
    return (single_out, pair_out, grad_single, grad_pair)


def solution(mesh):
    placed = (
        P("walk", ("row", "col"), None),
        P("walk", "row", "col", None),
        P(),
        P(),
        P(),
        P(),
        P(),
        P(),
        P("walk", ("row", "col"), None),
        P("walk", "row", "col", None),
    )
    return jax.shard_map(
        body,
        mesh=mesh,
        in_specs=placed,
        out_specs=(
            P("walk", ("row", "col"), None),
            P("walk", "row", "col", None),
            P("walk", ("row", "col"), None),
            P("walk", "row", "col", None),
        ),
        check_vma=False,
    )
```

```python
import jax
import jax.numpy as jnp
from jax import lax
from jax.experimental import pallas as pl
from jax.experimental.pallas import tpu as pltpu
from jax.sharding import PartitionSpec as P

def pair_kernel(pair_ref, dpair_ref, msg_ref, wp_ref, b_ref, mask_ref, aup_ref, adn_ref,
                *rest):
    out_ref, grad_ref, col_ref = rest[-3:]
    i = pl.program_id(1)
    ti, bc, dp = pair_ref.shape[1:]
    x = pair_ref[0]
    pre = jnp.dot(x.reshape(ti * bc, dp), wp_ref[...], preferred_element_type=jnp.float32)
    pre = pre.reshape(ti, bc, dp) + msg_ref[0][None] + b_ref[...][None]
    act = jnp.tanh(pre)
    out_ref[0] = (x.astype(jnp.float32) + act).astype(out_ref.dtype)
    d = dpair_ref[0].astype(jnp.float32)
    delta = (d * (1.0 - act * act)).astype(jnp.bfloat16)
    back = lax.dot_general(
        delta.reshape(ti * bc, dp), wp_ref[...], (((1,), (1,)), ((), ())),
        preferred_element_type=jnp.float32,
    )
    spread = jnp.where(mask_ref[...][None] > 0.5, aup_ref[0][:, None, :], adn_ref[0][:, None, :])
    grad_ref[0] = (d + back.reshape(ti, bc, dp) + spread).astype(grad_ref.dtype)
    part = jnp.sum(delta.astype(jnp.float32), axis=0)

    @pl.when(i == 0)
    def _():
        col_ref[0] = part

    @pl.when(i > 0)
    def _():
        col_ref[0] = col_ref[0] + part


def pair_pass(pair, d_pair, message_b, w_pair, b_pair, up_mask, a_up, a_down, first, prev=None):
    w, br, bc, dp = pair.shape
    group = message_b.shape[0]
    ti = max(1, min(br, 16384 // bc))
    grid = (group, br // ti)
    blk = pl.BlockSpec((1, ti, bc, dp), lambda a, i: (a + first, i, 0, 0))
    whole2 = lambda shape: pl.BlockSpec(shape, lambda a, i: (0, 0))
    per_w = pl.BlockSpec((1, bc, dp), lambda a, i: (a, 0, 0))
    rows = pl.BlockSpec((1, ti, dp), lambda a, i: (a, i, 0))
    in_specs = [blk, blk, per_w, whole2((dp, dp)), whole2((1, dp)),
                whole2((bc, 1)), rows, rows]
    args = [pair, d_pair, message_b, w_pair, b_pair.reshape(1, dp), up_mask, a_up, a_down]
    aliases = {}
    if prev is not None:
        in_specs += [pl.BlockSpec(memory_space=pl.ANY), pl.BlockSpec(memory_space=pl.ANY)]
        aliases = {len(args): 0, len(args) + 1: 1}
        args += list(prev)
    return pl.pallas_call(
        pair_kernel,
        grid=grid,
        in_specs=in_specs,
        out_specs=[blk, blk, per_w],
        out_shape=[jax.ShapeDtypeStruct(pair.shape, jnp.bfloat16),
                   jax.ShapeDtypeStruct(pair.shape, jnp.bfloat16),
                   jax.ShapeDtypeStruct((group, bc, dp), jnp.float32)],
        input_output_aliases=aliases,
        cost_estimate=pl.CostEstimate(
            flops=4 * group * br * bc * dp * dp,
            transcendentals=group * br * bc * dp,
            bytes_accessed=8 * group * br * bc * dp,
        ),
        compiler_params=pltpu.CompilerParams(dimension_semantics=("arbitrary", "arbitrary")),
    )(*args)


highest = lax.Precision.HIGHEST


def roll_pieces(pieces, shift):
    n = pieces.shape[0]
    doubled = jnp.concatenate([pieces, pieces], axis=0)
    return lax.dynamic_slice_in_dim(doubled, (n - shift) % n, n, 0)


def body(one_elec, pair, spins, w_single, b_single, w_pair, w_msg, b_pair, d_single, d_pair):
    walkers, block_rows, block_cols, width_pair = pair.shape
    own_rows = one_elec.shape[1]
    width_single = one_elec.shape[2]
    electrons = spins.shape[0]
    rows = electrons // block_rows
    cols = electrons // block_cols
    assert rows == cols
    pair_down = float(electrons) ** (-0.75)
    pair_boost = float(electrons) ** 0.75
    row_index = lax.axis_index("row")
    col_index = lax.axis_index("col")
    spin_up = spins.astype(jnp.float32)
    spin_down = 1.0 - spin_up
    count_up = jnp.sum(spin_up)
    count_down = float(electrons) - count_up
    spin_table = jnp.stack([spin_up, spin_down], axis=1)
    col_start = col_index * block_cols
    own_start = (row_index * cols + col_index) * own_rows
    col_table = lax.dynamic_slice_in_dim(spin_table, col_start, block_cols, 0)
    own_table = lax.dynamic_slice_in_dim(spin_table, own_start, own_rows, 0)

    both = ("row", "col")
    pieces = []
    for s in range(rows):
        perm = [(a * cols + b, ((b - s) % rows) * cols + a) for a in range(rows) for b in range(cols)]
        pieces.append(lax.ppermute(one_elec, both, perm))
    col_single = roll_pieces(jnp.stack(pieces), row_index)
    col_single = jnp.moveaxis(col_single, 0, 1).reshape(walkers, block_cols, width_single)

    col_spin_sums = jnp.einsum(
        "wjd,js->wsd", col_single, col_table.astype(jnp.bfloat16), preferred_element_type=jnp.float32
    )
    partial_value = jnp.einsum(
        "wijd,js->wisd", pair, col_table.astype(jnp.bfloat16), preferred_element_type=jnp.float32
    )
    sub_value = partial_value.reshape(walkers, cols, own_rows, 2, width_pair)
    own_sum = lax.dynamic_index_in_dim(sub_value, col_index, 1, keepdims=False)
    spin_sums = col_spin_sums
    spin_hi = col_spin_sums.astype(jnp.bfloat16)
    spin_lo = (col_spin_sums - spin_hi.astype(jnp.float32)).astype(jnp.bfloat16)
    split = own_rows * 2 * width_pair
    spin_size = 2 * width_single
    for s in range(1, cols):
        dest = col_index ^ s
        sent = lax.dynamic_index_in_dim(sub_value, dest, 1, keepdims=False)
        payload = jnp.concatenate(
            [
                sent.astype(jnp.bfloat16).reshape(walkers, -1),
                spin_hi.reshape(walkers, -1),
                spin_lo.reshape(walkers, -1),
            ],
            axis=1,
        )
        got = lax.ppermute(payload, "col", [(b, b ^ s) for b in range(cols)])
        own_sum = own_sum + got[:, :split].astype(jnp.float32).reshape(own_sum.shape)
        got_hi = got[:, split : split + spin_size].astype(jnp.float32)
        got_lo = got[:, split + spin_size :].astype(jnp.float32)
        spin_sums = spin_sums + (got_hi + got_lo).reshape(spin_sums.shape)

    single_wide = one_elec.astype(jnp.float32)
    features = jnp.concatenate(
        [
            single_wide,
            jnp.broadcast_to((spin_sums[:, 0, :] / count_up)[:, None], (walkers, own_rows, width_single)),
            jnp.broadcast_to((spin_sums[:, 1, :] / count_down)[:, None], (walkers, own_rows, width_single)),
            own_sum[:, :, 0, :] / count_up,
            own_sum[:, :, 1, :] / count_down,
        ],
        axis=2,
    ).astype(jnp.bfloat16)
    single_act = jnp.tanh(
        jnp.einsum("wif,fd->wid", features, w_single, preferred_element_type=jnp.float32) + b_single
    )
    single_out = (single_wide + single_act).astype(jnp.bfloat16)
    grad_pre = (d_single.astype(jnp.float32) * (1.0 - single_act * single_act)).astype(jnp.bfloat16)
    feature_grad = jnp.einsum("wid,fd->wif", grad_pre, w_single, preferred_element_type=jnp.float32)
    grad_direct = feature_grad[:, :, :width_single]
    grad_means = feature_grad[:, :, width_single : 3 * width_single].reshape(
        walkers, own_rows, 2, width_single
    )
    grad_pair_means = feature_grad[:, :, 3 * width_single :].reshape(
        walkers, own_rows, 2, width_pair
    )
    mean_sums = jnp.sum(grad_means, axis=1)

    mean_hi = mean_sums.astype(jnp.bfloat16)
    mean_lo = (mean_sums - mean_hi.astype(jnp.float32)).astype(jnp.bfloat16)
    payload = jnp.concatenate(
        [
            grad_pair_means.astype(jnp.bfloat16).reshape(walkers, -1),
            mean_hi.reshape(walkers, -1),
            mean_lo.reshape(walkers, -1),
        ],
        axis=1,
    )
    split = own_rows * 2 * width_pair
    mean_size = 2 * width_single
    gathered = [grad_pair_means.astype(jnp.bfloat16).astype(jnp.float32)] + [None] * (cols - 1)
    mean_part = mean_sums
    for s in range(1, cols):
        got = lax.ppermute(payload, "col", [(b, b ^ s) for b in range(cols)])
        gathered[s] = got[:, :split].astype(jnp.float32).reshape(grad_pair_means.shape)
        got_hi = got[:, split : split + mean_size].astype(jnp.float32)
        got_lo = got[:, split + mean_size :].astype(jnp.float32)
        mean_part = mean_part + (got_hi + got_lo).reshape(mean_sums.shape)
    ordered = []
    for m in range(cols):
        pick = gathered[0]
        for s in range(1, cols):
            pick = jnp.where((col_index ^ m) == s, gathered[s], pick)
        ordered.append(pick)
    row_pair_grads = jnp.stack(ordered, axis=1).reshape(walkers, block_rows, 2, width_pair)

    message = jnp.einsum("wjd,de->wje", col_single, w_msg, preferred_element_type=jnp.float32)
    a_up = pair_boost * (row_pair_grads[:, :, 0, :] / count_up)
    a_down = pair_boost * (row_pair_grads[:, :, 1, :] / count_down)
    up_mask = col_table[:, :1]
    pair_out, grad_pair, column_sum = pair_pass(
        pair, d_pair, message, w_pair, b_pair, up_mask, a_up, a_down, 0
    )

    sub_cols = column_sum.reshape(walkers, rows, own_rows, width_pair)
    mean_hi = mean_part.astype(jnp.bfloat16)
    mean_lo = (mean_part - mean_hi.astype(jnp.float32)).astype(jnp.bfloat16)
    split = own_rows * width_pair
    mean_size = 2 * width_single
    own_cols = None
    mean_total = None
    for s in range(rows):
        sent = lax.dynamic_index_in_dim(sub_cols, (row_index + s) % rows, 1, keepdims=False)
        payload = jnp.concatenate(
            [
                sent.astype(jnp.bfloat16).reshape(walkers, -1),
                mean_hi.reshape(walkers, -1),
                mean_lo.reshape(walkers, -1),
            ],
            axis=1,
        )
        perm = [(a * cols + b, b * cols + (a + s) % rows) for a in range(rows) for b in range(cols)]
        got = lax.ppermute(payload, both, perm)
        got_cols = got[:, :split].astype(jnp.float32).reshape(walkers, own_rows, width_pair)
        got_hi = got[:, split : split + mean_size].astype(jnp.float32)
        got_lo = got[:, split + mean_size :].astype(jnp.float32)
        got_mean = (got_hi + got_lo).reshape(mean_part.shape)
        own_cols = got_cols if own_cols is None else own_cols + got_cols
        mean_total = got_mean if mean_total is None else mean_total + got_mean

    own_message = pair_down * jnp.einsum(
        "wje,de->wjd", own_cols, w_msg.astype(jnp.float32), precision=highest
    )
    own_up = own_table[:, 0]
    own_down = own_table[:, 1]
    electron_grad = (
        own_up[None, :, None] * (mean_total[:, 0, :] / count_up)[:, None, :]
        + own_down[None, :, None] * (mean_total[:, 1, :] / count_down)[:, None, :]
        + own_message
    )
    grad_single = d_single.astype(jnp.float32) + grad_direct + electron_grad
    return (single_out, pair_out, grad_single, grad_pair)


def solution(mesh):
    placed = (
        P("walk", ("row", "col"), None),
        P("walk", "row", "col", None),
        P(),
        P(),
        P(),
        P(),
        P(),
        P(),
        P("walk", ("row", "col"), None),
        P("walk", "row", "col", None),
    )
    return jax.shard_map(
        body,
        mesh=mesh,
        in_specs=placed,
        out_specs=(
            P("walk", ("row", "col"), None),
            P("walk", "row", "col", None),
            P("walk", ("row", "col"), None),
            P("walk", "row", "col", None),
        ),
        check_vma=False,
    )
```

```python
import jax
import jax.numpy as jnp
from jax import lax
from jax.experimental import pallas as pl
from jax.experimental.pallas import tpu as pltpu
from jax.sharding import PartitionSpec as P

def pair_kernel(pair_ref, dpair_ref, msg_ref, wp_ref, b_ref, mask_ref, aup_ref, adn_ref,
                *rest):
    out_ref, grad_ref, col_ref = rest[-3:]
    i = pl.program_id(1)
    ti, bc, dp = pair_ref.shape[1:]
    x = pair_ref[0]
    pre = jnp.dot(x.reshape(ti * bc, dp), wp_ref[...], preferred_element_type=jnp.float32)
    pre = pre.reshape(ti, bc, dp) + msg_ref[0][None] + b_ref[...][None]
    act = jnp.tanh(pre)
    out_ref[0] = (x.astype(jnp.float32) + act).astype(out_ref.dtype)
    d = dpair_ref[0].astype(jnp.float32)
    delta = (d * (1.0 - act * act)).astype(jnp.bfloat16)
    back = lax.dot_general(
        delta.reshape(ti * bc, dp), wp_ref[...], (((1,), (1,)), ((), ())),
        preferred_element_type=jnp.float32,
    )
    spread = jnp.where(mask_ref[...][None] > 0.5, aup_ref[0][:, None, :], adn_ref[0][:, None, :])
    grad_ref[0] = (d + back.reshape(ti, bc, dp) + spread).astype(grad_ref.dtype)
    part = jnp.sum(delta.astype(jnp.float32), axis=0)

    @pl.when(i == 0)
    def _():
        col_ref[0] = part

    @pl.when(i > 0)
    def _():
        col_ref[0] = col_ref[0] + part


def pair_pass(pair, d_pair, message_b, w_pair, b_pair, up_mask, a_up, a_down, first, prev=None):
    w, br, bc, dp = pair.shape
    group = message_b.shape[0]
    ti = max(1, min(br, 8192 // bc))
    grid = (group, br // ti)
    blk = pl.BlockSpec((1, ti, bc, dp), lambda a, i: (a + first, i, 0, 0))
    whole2 = lambda shape: pl.BlockSpec(shape, lambda a, i: (0, 0))
    per_w = pl.BlockSpec((1, bc, dp), lambda a, i: (a, 0, 0))
    rows = pl.BlockSpec((1, ti, dp), lambda a, i: (a, i, 0))
    in_specs = [blk, blk, per_w, whole2((dp, dp)), whole2((1, dp)),
                whole2((bc, 1)), rows, rows]
    args = [pair, d_pair, message_b, w_pair, b_pair.reshape(1, dp), up_mask, a_up, a_down]
    aliases = {}
    if prev is not None:
        in_specs += [pl.BlockSpec(memory_space=pl.ANY), pl.BlockSpec(memory_space=pl.ANY)]
        aliases = {len(args): 0, len(args) + 1: 1}
        args += list(prev)
    return pl.pallas_call(
        pair_kernel,
        grid=grid,
        in_specs=in_specs,
        out_specs=[blk, blk, per_w],
        out_shape=[jax.ShapeDtypeStruct(pair.shape, jnp.bfloat16),
                   jax.ShapeDtypeStruct(pair.shape, jnp.bfloat16),
                   jax.ShapeDtypeStruct((group, bc, dp), jnp.float32)],
        input_output_aliases=aliases,
        cost_estimate=pl.CostEstimate(
            flops=4 * group * br * bc * dp * dp,
            transcendentals=group * br * bc * dp,
            bytes_accessed=8 * group * br * bc * dp,
        ),
        compiler_params=pltpu.CompilerParams(dimension_semantics=("arbitrary", "arbitrary")),
    )(*args)


highest = lax.Precision.HIGHEST


def roll_pieces(pieces, shift):
    n = pieces.shape[0]
    doubled = jnp.concatenate([pieces, pieces], axis=0)
    return lax.dynamic_slice_in_dim(doubled, (n - shift) % n, n, 0)


def body(one_elec, pair, spins, w_single, b_single, w_pair, w_msg, b_pair, d_single, d_pair):
    walkers, block_rows, block_cols, width_pair = pair.shape
    own_rows = one_elec.shape[1]
    width_single = one_elec.shape[2]
    electrons = spins.shape[0]
    rows = electrons // block_rows
    cols = electrons // block_cols
    assert rows == cols
    pair_down = float(electrons) ** (-0.75)
    pair_boost = float(electrons) ** 0.75
    row_index = lax.axis_index("row")
    col_index = lax.axis_index("col")
    spin_up = spins.astype(jnp.float32)
    spin_down = 1.0 - spin_up
    count_up = jnp.sum(spin_up)
    count_down = float(electrons) - count_up
    spin_table = jnp.stack([spin_up, spin_down], axis=1)
    col_start = col_index * block_cols
    own_start = (row_index * cols + col_index) * own_rows
    col_table = lax.dynamic_slice_in_dim(spin_table, col_start, block_cols, 0)
    own_table = lax.dynamic_slice_in_dim(spin_table, own_start, own_rows, 0)

    both = ("row", "col")
    pieces = []
    for s in range(rows):
        perm = [(a * cols + b, ((b - s) % rows) * cols + a) for a in range(rows) for b in range(cols)]
        pieces.append(lax.ppermute(one_elec, both, perm))
    col_single = roll_pieces(jnp.stack(pieces), row_index)
    col_single = jnp.moveaxis(col_single, 0, 1).reshape(walkers, block_cols, width_single)

    col_spin_sums = jnp.einsum(
        "wjd,js->wsd", col_single, col_table.astype(jnp.bfloat16), preferred_element_type=jnp.float32
    )
    partial_value = jnp.einsum(
        "wijd,js->wisd", pair, col_table.astype(jnp.bfloat16), preferred_element_type=jnp.float32
    )
    sub_value = partial_value.reshape(walkers, cols, own_rows, 2, width_pair)
    own_sum = lax.dynamic_index_in_dim(sub_value, col_index, 1, keepdims=False)
    spin_sums = col_spin_sums
    spin_hi = col_spin_sums.astype(jnp.bfloat16)
    spin_lo = (col_spin_sums - spin_hi.astype(jnp.float32)).astype(jnp.bfloat16)
    split = own_rows * 2 * width_pair
    spin_size = 2 * width_single
    for s in range(cols - 1, 0, -1):
        dest = col_index ^ s
        sent = lax.dynamic_index_in_dim(sub_value, dest, 1, keepdims=False)
        payload = jnp.concatenate(
            [
                sent.astype(jnp.bfloat16).reshape(walkers, -1),
                spin_hi.reshape(walkers, -1),
                spin_lo.reshape(walkers, -1),
            ],
            axis=1,
        )
        got = lax.ppermute(payload, "col", [(b, b ^ s) for b in range(cols)])
        own_sum = own_sum + got[:, :split].astype(jnp.float32).reshape(own_sum.shape)
        got_hi = got[:, split : split + spin_size].astype(jnp.float32)
        got_lo = got[:, split + spin_size :].astype(jnp.float32)
        spin_sums = spin_sums + (got_hi + got_lo).reshape(spin_sums.shape)

    single_wide = one_elec.astype(jnp.float32)
    features = jnp.concatenate(
        [
            single_wide,
            jnp.broadcast_to((spin_sums[:, 0, :] / count_up)[:, None], (walkers, own_rows, width_single)),
            jnp.broadcast_to((spin_sums[:, 1, :] / count_down)[:, None], (walkers, own_rows, width_single)),
            own_sum[:, :, 0, :] / count_up,
            own_sum[:, :, 1, :] / count_down,
        ],
        axis=2,
    ).astype(jnp.bfloat16)
    single_act = jnp.tanh(
        jnp.einsum("wif,fd->wid", features, w_single, preferred_element_type=jnp.float32) + b_single
    )
    single_out = (single_wide + single_act).astype(jnp.bfloat16)
    grad_pre = (d_single.astype(jnp.float32) * (1.0 - single_act * single_act)).astype(jnp.bfloat16)
    feature_grad = jnp.einsum("wid,fd->wif", grad_pre, w_single, preferred_element_type=jnp.float32)
    grad_direct = feature_grad[:, :, :width_single]
    grad_means = feature_grad[:, :, width_single : 3 * width_single].reshape(
        walkers, own_rows, 2, width_single
    )
    grad_pair_means = feature_grad[:, :, 3 * width_single :].reshape(
        walkers, own_rows, 2, width_pair
    )
    mean_sums = jnp.sum(grad_means, axis=1)

    mean_hi = mean_sums.astype(jnp.bfloat16)
    mean_lo = (mean_sums - mean_hi.astype(jnp.float32)).astype(jnp.bfloat16)
    payload = jnp.concatenate(
        [
            grad_pair_means.astype(jnp.bfloat16).reshape(walkers, -1),
            mean_hi.reshape(walkers, -1),
            mean_lo.reshape(walkers, -1),
        ],
        axis=1,
    )
    split = own_rows * 2 * width_pair
    mean_size = 2 * width_single
    gathered = [grad_pair_means.astype(jnp.bfloat16).astype(jnp.float32)] + [None] * (cols - 1)
    mean_part = mean_sums
    for s in range(cols - 1, 0, -1):
        got = lax.ppermute(payload, "col", [(b, b ^ s) for b in range(cols)])
        gathered[s] = got[:, :split].astype(jnp.float32).reshape(grad_pair_means.shape)
        got_hi = got[:, split : split + mean_size].astype(jnp.float32)
        got_lo = got[:, split + mean_size :].astype(jnp.float32)
        mean_part = mean_part + (got_hi + got_lo).reshape(mean_sums.shape)
    ordered = []
    for m in range(cols):
        pick = gathered[0]
        for s in range(cols - 1, 0, -1):
            pick = jnp.where((col_index ^ m) == s, gathered[s], pick)
        ordered.append(pick)
    row_pair_grads = jnp.stack(ordered, axis=1).reshape(walkers, block_rows, 2, width_pair)

    message = jnp.einsum("wjd,de->wje", col_single, w_msg, preferred_element_type=jnp.float32)
    a_up = pair_boost * (row_pair_grads[:, :, 0, :] / count_up)
    a_down = pair_boost * (row_pair_grads[:, :, 1, :] / count_down)
    up_mask = col_table[:, :1]
    pair_out, grad_pair, column_sum = pair_pass(
        pair, d_pair, message, w_pair, b_pair, up_mask, a_up, a_down, 0
    )

    sub_cols = column_sum.reshape(walkers, rows, own_rows, width_pair)
    mean_hi = mean_part.astype(jnp.bfloat16)
    mean_lo = (mean_part - mean_hi.astype(jnp.float32)).astype(jnp.bfloat16)
    split = own_rows * width_pair
    mean_size = 2 * width_single
    own_cols = None
    mean_total = None
    for s in range(rows):
        sent = lax.dynamic_index_in_dim(sub_cols, (row_index + s) % rows, 1, keepdims=False)
        payload = jnp.concatenate(
            [
                sent.astype(jnp.bfloat16).reshape(walkers, -1),
                mean_hi.reshape(walkers, -1),
                mean_lo.reshape(walkers, -1),
            ],
            axis=1,
        )
        perm = [(a * cols + b, b * cols + (a + s) % rows) for a in range(rows) for b in range(cols)]
        got = lax.ppermute(payload, both, perm)
        got_cols = got[:, :split].astype(jnp.float32).reshape(walkers, own_rows, width_pair)
        got_hi = got[:, split : split + mean_size].astype(jnp.float32)
        got_lo = got[:, split + mean_size :].astype(jnp.float32)
        got_mean = (got_hi + got_lo).reshape(mean_part.shape)
        own_cols = got_cols if own_cols is None else own_cols + got_cols
        mean_total = got_mean if mean_total is None else mean_total + got_mean

    own_message = pair_down * jnp.einsum(
        "wje,de->wjd", own_cols, w_msg.astype(jnp.float32), precision=highest
    )
    own_up = own_table[:, 0]
    own_down = own_table[:, 1]
    electron_grad = (
        own_up[None, :, None] * (mean_total[:, 0, :] / count_up)[:, None, :]
        + own_down[None, :, None] * (mean_total[:, 1, :] / count_down)[:, None, :]
        + own_message
    )
    grad_single = d_single.astype(jnp.float32) + grad_direct + electron_grad
    return (single_out, pair_out, grad_single, grad_pair)


def solution(mesh):
    placed = (
        P("walk", ("row", "col"), None),
        P("walk", "row", "col", None),
        P(),
        P(),
        P(),
        P(),
        P(),
        P(),
        P("walk", ("row", "col"), None),
        P("walk", "row", "col", None),
    )
    return jax.shard_map(
        body,
        mesh=mesh,
        in_specs=placed,
        out_specs=(
            P("walk", ("row", "col"), None),
            P("walk", "row", "col", None),
            P("walk", ("row", "col"), None),
            P("walk", "row", "col", None),
        ),
        check_vma=False,
    )
```

```python
import jax
import jax.numpy as jnp
from jax import lax
from jax.experimental import pallas as pl
from jax.experimental.pallas import tpu as pltpu
from jax.sharding import PartitionSpec as P

def pair_kernel(pair_ref, dpair_ref, msg_ref, wp_ref, b_ref, mask_ref, aup_ref, adn_ref,
                *rest):
    out_ref, grad_ref, col_ref = rest[-3:]
    i = pl.program_id(1)
    ti, bc, dp = pair_ref.shape[1:]
    x = pair_ref[0]
    pre = jnp.dot(x.reshape(ti * bc, dp), wp_ref[...], preferred_element_type=jnp.float32)
    pre = pre.reshape(ti, bc, dp) + msg_ref[0][None] + b_ref[...][None]
    act = jnp.tanh(pre)
    out_ref[0] = (x.astype(jnp.float32) + act).astype(out_ref.dtype)
    d = dpair_ref[0].astype(jnp.float32)
    delta = (d * (1.0 - act * act)).astype(jnp.bfloat16)
    back = lax.dot_general(
        delta.reshape(ti * bc, dp), wp_ref[...], (((1,), (1,)), ((), ())),
        preferred_element_type=jnp.float32,
    )
    spread = jnp.where(mask_ref[...][None] > 0.5, aup_ref[0][:, None, :], adn_ref[0][:, None, :])
    grad_ref[0] = (d + back.reshape(ti, bc, dp) + spread).astype(grad_ref.dtype)
    part = jnp.sum(delta.astype(jnp.float32), axis=0)

    @pl.when(i == 0)
    def _():
        col_ref[0] = part

    @pl.when(i > 0)
    def _():
        col_ref[0] = col_ref[0] + part


def pair_pass(pair, d_pair, message_b, w_pair, b_pair, up_mask, a_up, a_down, first, prev=None):
    w, br, bc, dp = pair.shape
    group = message_b.shape[0]
    ti = max(1, min(br, 16384 // bc))
    grid = (group, br // ti)
    blk = pl.BlockSpec((1, ti, bc, dp), lambda a, i: (a + first, i, 0, 0))
    whole2 = lambda shape: pl.BlockSpec(shape, lambda a, i: (0, 0))
    per_w = pl.BlockSpec((1, bc, dp), lambda a, i: (a, 0, 0))
    rows = pl.BlockSpec((1, ti, dp), lambda a, i: (a, i, 0))
    in_specs = [blk, blk, per_w, whole2((dp, dp)), whole2((1, dp)),
                whole2((bc, 1)), rows, rows]
    args = [pair, d_pair, message_b, w_pair, b_pair.reshape(1, dp), up_mask, a_up, a_down]
    aliases = {}
    if prev is not None:
        in_specs += [pl.BlockSpec(memory_space=pl.ANY), pl.BlockSpec(memory_space=pl.ANY)]
        aliases = {len(args): 0, len(args) + 1: 1}
        args += list(prev)
    return pl.pallas_call(
        pair_kernel,
        grid=grid,
        in_specs=in_specs,
        out_specs=[blk, blk, per_w],
        out_shape=[jax.ShapeDtypeStruct(pair.shape, jnp.bfloat16),
                   jax.ShapeDtypeStruct(pair.shape, jnp.bfloat16),
                   jax.ShapeDtypeStruct((group, bc, dp), jnp.float32)],
        input_output_aliases=aliases,
        cost_estimate=pl.CostEstimate(
            flops=4 * group * br * bc * dp * dp,
            transcendentals=group * br * bc * dp,
            bytes_accessed=8 * group * br * bc * dp,
        ),
        compiler_params=pltpu.CompilerParams(dimension_semantics=("arbitrary", "arbitrary")),
    )(*args)


highest = lax.Precision.HIGHEST


def roll_pieces(pieces, shift):
    n = pieces.shape[0]
    doubled = jnp.concatenate([pieces, pieces], axis=0)
    return lax.dynamic_slice_in_dim(doubled, (n - shift) % n, n, 0)


def body(one_elec, pair, spins, w_single, b_single, w_pair, w_msg, b_pair, d_single, d_pair):
    walkers, block_rows, block_cols, width_pair = pair.shape
    own_rows = one_elec.shape[1]
    width_single = one_elec.shape[2]
    electrons = spins.shape[0]
    rows = electrons // block_rows
    cols = electrons // block_cols
    assert rows == cols
    pair_down = float(electrons) ** (-0.75)
    pair_boost = float(electrons) ** 0.75
    row_index = lax.axis_index("row")
    col_index = lax.axis_index("col")
    spin_up = spins.astype(jnp.float32)
    spin_down = 1.0 - spin_up
    count_up = jnp.sum(spin_up)
    count_down = float(electrons) - count_up
    spin_table = jnp.stack([spin_up, spin_down], axis=1)
    col_start = col_index * block_cols
    own_start = (row_index * cols + col_index) * own_rows
    col_table = lax.dynamic_slice_in_dim(spin_table, col_start, block_cols, 0)
    own_table = lax.dynamic_slice_in_dim(spin_table, own_start, own_rows, 0)

    both = ("row", "col")
    pieces = []
    for s in range(rows):
        perm = [(a * cols + b, ((b - s) % rows) * cols + a) for a in range(rows) for b in range(cols)]
        pieces.append(lax.ppermute(one_elec, both, perm))
    col_single = roll_pieces(jnp.stack(pieces), row_index)
    col_single = jnp.moveaxis(col_single, 0, 1).reshape(walkers, block_cols, width_single)

    col_spin_sums = jnp.einsum(
        "wjd,js->wsd", col_single, col_table.astype(jnp.bfloat16), preferred_element_type=jnp.float32
    )
    partial_value = jnp.einsum(
        "wijd,js->wisd", pair, col_table.astype(jnp.bfloat16), preferred_element_type=jnp.float32
    )
    sub_value = partial_value.reshape(walkers, cols, own_rows, 2, width_pair)
    own_sum = lax.dynamic_index_in_dim(sub_value, col_index, 1, keepdims=False)
    spin_sums = col_spin_sums
    spin_hi = col_spin_sums.astype(jnp.bfloat16)
    spin_lo = (col_spin_sums - spin_hi.astype(jnp.float32)).astype(jnp.bfloat16)
    split = own_rows * 2 * width_pair
    spin_size = 2 * width_single
    for s in range(cols - 1, 0, -1):
        dest = col_index ^ s
        sent = lax.dynamic_index_in_dim(sub_value, dest, 1, keepdims=False)
        payload = jnp.concatenate(
            [
                sent.astype(jnp.bfloat16).reshape(walkers, -1),
                spin_hi.reshape(walkers, -1),
                spin_lo.reshape(walkers, -1),
            ],
            axis=1,
        )
        got = lax.ppermute(payload, "col", [(b, b ^ s) for b in range(cols)])
        own_sum = own_sum + got[:, :split].astype(jnp.float32).reshape(own_sum.shape)
        got_hi = got[:, split : split + spin_size].astype(jnp.float32)
        got_lo = got[:, split + spin_size :].astype(jnp.float32)
        spin_sums = spin_sums + (got_hi + got_lo).reshape(spin_sums.shape)

    single_wide = one_elec.astype(jnp.float32)
    features = jnp.concatenate(
        [
            single_wide,
            jnp.broadcast_to((spin_sums[:, 0, :] / count_up)[:, None], (walkers, own_rows, width_single)),
            jnp.broadcast_to((spin_sums[:, 1, :] / count_down)[:, None], (walkers, own_rows, width_single)),
            own_sum[:, :, 0, :] / count_up,
            own_sum[:, :, 1, :] / count_down,
        ],
        axis=2,
    ).astype(jnp.bfloat16)
    single_act = jnp.tanh(
        jnp.einsum("wif,fd->wid", features, w_single, preferred_element_type=jnp.float32) + b_single
    )
    single_out = (single_wide + single_act).astype(jnp.bfloat16)
    grad_pre = (d_single.astype(jnp.float32) * (1.0 - single_act * single_act)).astype(jnp.bfloat16)
    feature_grad = jnp.einsum("wid,fd->wif", grad_pre, w_single, preferred_element_type=jnp.float32)
    grad_direct = feature_grad[:, :, :width_single]
    grad_means = feature_grad[:, :, width_single : 3 * width_single].reshape(
        walkers, own_rows, 2, width_single
    )
    grad_pair_means = feature_grad[:, :, 3 * width_single :].reshape(
        walkers, own_rows, 2, width_pair
    )
    mean_sums = jnp.sum(grad_means, axis=1)

    mean_hi = mean_sums.astype(jnp.bfloat16)
    mean_lo = (mean_sums - mean_hi.astype(jnp.float32)).astype(jnp.bfloat16)
    payload = jnp.concatenate(
        [
            grad_pair_means.astype(jnp.bfloat16).reshape(walkers, -1),
            mean_hi.reshape(walkers, -1),
            mean_lo.reshape(walkers, -1),
        ],
        axis=1,
    )
    split = own_rows * 2 * width_pair
    mean_size = 2 * width_single
    gathered = [grad_pair_means.astype(jnp.bfloat16).astype(jnp.float32)] + [None] * (cols - 1)
    mean_part = mean_sums
    for s in range(cols - 1, 0, -1):
        got = lax.ppermute(payload, "col", [(b, b ^ s) for b in range(cols)])
        gathered[s] = got[:, :split].astype(jnp.float32).reshape(grad_pair_means.shape)
        got_hi = got[:, split : split + mean_size].astype(jnp.float32)
        got_lo = got[:, split + mean_size :].astype(jnp.float32)
        mean_part = mean_part + (got_hi + got_lo).reshape(mean_sums.shape)
    ordered = []
    for m in range(cols):
        pick = gathered[0]
        for s in range(cols - 1, 0, -1):
            pick = jnp.where((col_index ^ m) == s, gathered[s], pick)
        ordered.append(pick)
    row_pair_grads = jnp.stack(ordered, axis=1).reshape(walkers, block_rows, 2, width_pair)

    message = jnp.einsum("wjd,de->wje", col_single, w_msg, preferred_element_type=jnp.float32)
    a_up = pair_boost * (row_pair_grads[:, :, 0, :] / count_up)
    a_down = pair_boost * (row_pair_grads[:, :, 1, :] / count_down)
    up_mask = col_table[:, :1]
    pair_out, grad_pair, column_sum = pair_pass(
        pair, d_pair, message, w_pair, b_pair, up_mask, a_up, a_down, 0
    )

    sub_cols = column_sum.reshape(walkers, rows, own_rows, width_pair)
    mean_hi = mean_part.astype(jnp.bfloat16)
    mean_lo = (mean_part - mean_hi.astype(jnp.float32)).astype(jnp.bfloat16)
    split = own_rows * width_pair
    mean_size = 2 * width_single
    own_cols = None
    mean_total = None
    for s in range(rows):
        sent = lax.dynamic_index_in_dim(sub_cols, (row_index + s) % rows, 1, keepdims=False)
        payload = jnp.concatenate(
            [
                sent.astype(jnp.bfloat16).reshape(walkers, -1),
                mean_hi.reshape(walkers, -1),
                mean_lo.reshape(walkers, -1),
            ],
            axis=1,
        )
        perm = [(a * cols + b, b * cols + (a + s) % rows) for a in range(rows) for b in range(cols)]
        got = lax.ppermute(payload, both, perm)
        got_cols = got[:, :split].astype(jnp.float32).reshape(walkers, own_rows, width_pair)
        got_hi = got[:, split : split + mean_size].astype(jnp.float32)
        got_lo = got[:, split + mean_size :].astype(jnp.float32)
        got_mean = (got_hi + got_lo).reshape(mean_part.shape)
        own_cols = got_cols if own_cols is None else own_cols + got_cols
        mean_total = got_mean if mean_total is None else mean_total + got_mean

    own_message = pair_down * jnp.einsum(
        "wje,de->wjd", own_cols, w_msg.astype(jnp.float32), precision=highest
    )
    own_up = own_table[:, 0]
    own_down = own_table[:, 1]
    electron_grad = (
        own_up[None, :, None] * (mean_total[:, 0, :] / count_up)[:, None, :]
        + own_down[None, :, None] * (mean_total[:, 1, :] / count_down)[:, None, :]
        + own_message
    )
    grad_single = d_single.astype(jnp.float32) + grad_direct + electron_grad
    return (single_out, pair_out, grad_single, grad_pair)


def solution(mesh):
    placed = (
        P("walk", ("row", "col"), None),
        P("walk", "row", "col", None),
        P(),
        P(),
        P(),
        P(),
        P(),
        P(),
        P("walk", ("row", "col"), None),
        P("walk", "row", "col", None),
    )
    return jax.shard_map(
        body,
        mesh=mesh,
        in_specs=placed,
        out_specs=(
            P("walk", ("row", "col"), None),
            P("walk", "row", "col", None),
            P("walk", ("row", "col"), None),
            P("walk", "row", "col", None),
        ),
        check_vma=False,
    )
```

```python
import jax
import jax.numpy as jnp
from jax import lax
from jax.experimental import pallas as pl
from jax.experimental.pallas import tpu as pltpu
from jax.sharding import PartitionSpec as P

def pair_kernel(pair_ref, dpair_ref, msg_ref, wp_ref, b_ref, mask_ref, aup_ref, adn_ref,
                *rest):
    out_ref, grad_ref, col_ref = rest[-3:]
    i = pl.program_id(1)
    ti, bc, dp = pair_ref.shape[1:]
    x = pair_ref[0]
    pre = jnp.dot(x.reshape(ti * bc, dp), wp_ref[...], preferred_element_type=jnp.float32)
    pre = pre.reshape(ti, bc, dp) + msg_ref[0][None] + b_ref[...][None]
    act = jnp.tanh(pre)
    out_ref[0] = (x.astype(jnp.float32) + act).astype(out_ref.dtype)
    d = dpair_ref[0].astype(jnp.float32)
    delta = (d * (1.0 - act * act)).astype(jnp.bfloat16)
    back = lax.dot_general(
        delta.reshape(ti * bc, dp), wp_ref[...], (((1,), (1,)), ((), ())),
        preferred_element_type=jnp.float32,
    )
    spread = jnp.where(mask_ref[...][None] > 0.5, aup_ref[0][:, None, :], adn_ref[0][:, None, :])
    grad_ref[0] = (d + back.reshape(ti, bc, dp) + spread).astype(grad_ref.dtype)
    part = jnp.sum(delta.astype(jnp.float32), axis=0)

    @pl.when(i == 0)
    def _():
        col_ref[0] = part

    @pl.when(i > 0)
    def _():
        col_ref[0] = col_ref[0] + part


def pair_pass(pair, d_pair, message_b, w_pair, b_pair, up_mask, a_up, a_down, first, prev=None):
    w, br, bc, dp = pair.shape
    group = message_b.shape[0]
    ti = max(1, min(br, 8192 // bc))
    grid = (group, br // ti)
    blk = pl.BlockSpec((1, ti, bc, dp), lambda a, i: (a + first, i, 0, 0))
    whole2 = lambda shape: pl.BlockSpec(shape, lambda a, i: (0, 0))
    per_w = pl.BlockSpec((1, bc, dp), lambda a, i: (a, 0, 0))
    rows = pl.BlockSpec((1, ti, dp), lambda a, i: (a, i, 0))
    in_specs = [blk, blk, per_w, whole2((dp, dp)), whole2((1, dp)),
                whole2((bc, 1)), rows, rows]
    args = [pair, d_pair, message_b, w_pair, b_pair.reshape(1, dp), up_mask, a_up, a_down]
    aliases = {}
    if prev is not None:
        in_specs += [pl.BlockSpec(memory_space=pl.ANY), pl.BlockSpec(memory_space=pl.ANY)]
        aliases = {len(args): 0, len(args) + 1: 1}
        args += list(prev)
    return pl.pallas_call(
        pair_kernel,
        grid=grid,
        in_specs=in_specs,
        out_specs=[blk, blk, per_w],
        out_shape=[jax.ShapeDtypeStruct(pair.shape, jnp.bfloat16),
                   jax.ShapeDtypeStruct(pair.shape, jnp.bfloat16),
                   jax.ShapeDtypeStruct((group, bc, dp), jnp.float32)],
        input_output_aliases=aliases,
        cost_estimate=pl.CostEstimate(
            flops=4 * group * br * bc * dp * dp,
            transcendentals=group * br * bc * dp,
            bytes_accessed=8 * group * br * bc * dp,
        ),
        compiler_params=pltpu.CompilerParams(dimension_semantics=("arbitrary", "arbitrary")),
    )(*args)


highest = lax.Precision.HIGHEST


def roll_pieces(pieces, shift):
    n = pieces.shape[0]
    doubled = jnp.concatenate([pieces, pieces], axis=0)
    return lax.dynamic_slice_in_dim(doubled, (n - shift) % n, n, 0)


def body(one_elec, pair, spins, w_single, b_single, w_pair, w_msg, b_pair, d_single, d_pair):
    walkers, block_rows, block_cols, width_pair = pair.shape
    own_rows = one_elec.shape[1]
    width_single = one_elec.shape[2]
    electrons = spins.shape[0]
    rows = electrons // block_rows
    cols = electrons // block_cols
    assert rows == cols
    pair_down = float(electrons) ** (-0.75)
    pair_boost = float(electrons) ** 0.75
    row_index = lax.axis_index("row")
    col_index = lax.axis_index("col")
    spin_up = spins.astype(jnp.float32)
    spin_down = 1.0 - spin_up
    count_up = jnp.sum(spin_up)
    count_down = float(electrons) - count_up
    spin_table = jnp.stack([spin_up, spin_down], axis=1)
    col_start = col_index * block_cols
    own_start = (row_index * cols + col_index) * own_rows
    col_table = lax.dynamic_slice_in_dim(spin_table, col_start, block_cols, 0)
    own_table = lax.dynamic_slice_in_dim(spin_table, own_start, own_rows, 0)

    both = ("row", "col")
    pieces = []
    for s in range(rows):
        perm = [(a * cols + b, ((b - s) % rows) * cols + a) for a in range(rows) for b in range(cols)]
        pieces.append(lax.ppermute(one_elec, both, perm))
    col_single = roll_pieces(jnp.stack(pieces), row_index)
    col_single = jnp.moveaxis(col_single, 0, 1).reshape(walkers, block_cols, width_single)

    col_spin_sums = jnp.einsum(
        "wjd,js->wsd", col_single, col_table.astype(jnp.bfloat16), preferred_element_type=jnp.float32
    )
    partial_value = jnp.einsum(
        "wijd,js->wisd", pair, col_table.astype(jnp.bfloat16), preferred_element_type=jnp.float32
    )
    sub_value = partial_value.reshape(walkers, cols, own_rows, 2, width_pair)
    own_sum = lax.dynamic_index_in_dim(sub_value, col_index, 1, keepdims=False)
    spin_sums = col_spin_sums
    spin_hi = col_spin_sums.astype(jnp.bfloat16)
    spin_lo = (col_spin_sums - spin_hi.astype(jnp.float32)).astype(jnp.bfloat16)
    split = own_rows * 2 * width_pair
    spin_size = 2 * width_single
    for s in range(cols - 1, 0, -1):
        dest = col_index ^ s
        sent = lax.dynamic_index_in_dim(sub_value, dest, 1, keepdims=False)
        payload = jnp.concatenate(
            [
                sent.astype(jnp.bfloat16).reshape(walkers, -1),
                spin_hi.reshape(walkers, -1),
                spin_lo.reshape(walkers, -1),
            ],
            axis=1,
        )
        got = lax.ppermute(payload, "col", [(b, b ^ s) for b in range(cols)])
        own_sum = own_sum + got[:, :split].astype(jnp.float32).reshape(own_sum.shape)
        got_hi = got[:, split : split + spin_size].astype(jnp.float32)
        got_lo = got[:, split + spin_size :].astype(jnp.float32)
        spin_sums = spin_sums + (got_hi + got_lo).reshape(spin_sums.shape)

    single_wide = one_elec.astype(jnp.float32)
    features = jnp.concatenate(
        [
            single_wide,
            jnp.broadcast_to((spin_sums[:, 0, :] / count_up)[:, None], (walkers, own_rows, width_single)),
            jnp.broadcast_to((spin_sums[:, 1, :] / count_down)[:, None], (walkers, own_rows, width_single)),
            own_sum[:, :, 0, :] / count_up,
            own_sum[:, :, 1, :] / count_down,
        ],
        axis=2,
    ).astype(jnp.bfloat16)
    single_act = jnp.tanh(
        jnp.einsum("wif,fd->wid", features, w_single, preferred_element_type=jnp.float32) + b_single
    )
    single_out = (single_wide + single_act).astype(jnp.bfloat16)
    grad_pre = (d_single.astype(jnp.float32) * (1.0 - single_act * single_act)).astype(jnp.bfloat16)
    feature_grad = jnp.einsum("wid,fd->wif", grad_pre, w_single, preferred_element_type=jnp.float32)
    grad_direct = feature_grad[:, :, :width_single]
    grad_means = feature_grad[:, :, width_single : 3 * width_single].reshape(
        walkers, own_rows, 2, width_single
    )
    grad_pair_means = feature_grad[:, :, 3 * width_single :].reshape(
        walkers, own_rows, 2, width_pair
    )
    mean_sums = jnp.sum(grad_means, axis=1)

    mean_hi = mean_sums.astype(jnp.bfloat16)
    mean_lo = (mean_sums - mean_hi.astype(jnp.float32)).astype(jnp.bfloat16)
    payload = jnp.concatenate(
        [
            grad_pair_means.astype(jnp.bfloat16).reshape(walkers, -1),
            mean_hi.reshape(walkers, -1),
            mean_lo.reshape(walkers, -1),
        ],
        axis=1,
    )
    split = own_rows * 2 * width_pair
    mean_size = 2 * width_single
    gathered = [grad_pair_means.astype(jnp.bfloat16).astype(jnp.float32)] + [None] * (cols - 1)
    mean_part = mean_sums
    for s in range(cols - 1, 0, -1):
        got = lax.ppermute(payload, "col", [(b, b ^ s) for b in range(cols)])
        gathered[s] = got[:, :split].astype(jnp.float32).reshape(grad_pair_means.shape)
        got_hi = got[:, split : split + mean_size].astype(jnp.float32)
        got_lo = got[:, split + mean_size :].astype(jnp.float32)
        mean_part = mean_part + (got_hi + got_lo).reshape(mean_sums.shape)
    ordered = []
    for m in range(cols):
        pick = gathered[0]
        for s in range(cols - 1, 0, -1):
            pick = jnp.where((col_index ^ m) == s, gathered[s], pick)
        ordered.append(pick)
    row_pair_grads = jnp.stack(ordered, axis=1).reshape(walkers, block_rows, 2, width_pair)

    message = jnp.einsum("wjd,de->wje", col_single, w_msg, preferred_element_type=jnp.float32)
    a_up = pair_boost * (row_pair_grads[:, :, 0, :] / count_up)
    a_down = pair_boost * (row_pair_grads[:, :, 1, :] / count_down)
    up_mask = col_table[:, :1]
    pair_out, grad_pair, column_sum = pair_pass(
        pair, d_pair, message, w_pair, b_pair, up_mask, a_up, a_down, 0
    )

    sub_cols = column_sum.reshape(walkers, rows, own_rows, width_pair)
    mean_hi = mean_part.astype(jnp.bfloat16)
    mean_lo = (mean_part - mean_hi.astype(jnp.float32)).astype(jnp.bfloat16)
    split = own_rows * width_pair
    mean_size = 2 * width_single
    own_cols = None
    mean_total = None
    for s in range(rows - 1, -1, -1):
        sent = lax.dynamic_index_in_dim(sub_cols, (row_index + s) % rows, 1, keepdims=False)
        payload = jnp.concatenate(
            [
                sent.astype(jnp.bfloat16).reshape(walkers, -1),
                mean_hi.reshape(walkers, -1),
                mean_lo.reshape(walkers, -1),
            ],
            axis=1,
        )
        perm = [(a * cols + b, b * cols + (a + s) % rows) for a in range(rows) for b in range(cols)]
        got = lax.ppermute(payload, both, perm)
        got_cols = got[:, :split].astype(jnp.float32).reshape(walkers, own_rows, width_pair)
        got_hi = got[:, split : split + mean_size].astype(jnp.float32)
        got_lo = got[:, split + mean_size :].astype(jnp.float32)
        got_mean = (got_hi + got_lo).reshape(mean_part.shape)
        own_cols = got_cols if own_cols is None else own_cols + got_cols
        mean_total = got_mean if mean_total is None else mean_total + got_mean

    own_message = pair_down * jnp.einsum(
        "wje,de->wjd", own_cols, w_msg.astype(jnp.float32), precision=highest
    )
    own_up = own_table[:, 0]
    own_down = own_table[:, 1]
    electron_grad = (
        own_up[None, :, None] * (mean_total[:, 0, :] / count_up)[:, None, :]
        + own_down[None, :, None] * (mean_total[:, 1, :] / count_down)[:, None, :]
        + own_message
    )
    grad_single = d_single.astype(jnp.float32) + grad_direct + electron_grad
    return (single_out, pair_out, grad_single, grad_pair)


def solution(mesh):
    placed = (
        P("walk", ("row", "col"), None),
        P("walk", "row", "col", None),
        P(),
        P(),
        P(),
        P(),
        P(),
        P(),
        P("walk", ("row", "col"), None),
        P("walk", "row", "col", None),
    )
    return jax.shard_map(
        body,
        mesh=mesh,
        in_specs=placed,
        out_specs=(
            P("walk", ("row", "col"), None),
            P("walk", "row", "col", None),
            P("walk", ("row", "col"), None),
            P("walk", "row", "col", None),
        ),
        check_vma=False,
    )
```
